128 devices in a mesh: dp: 8 (over x_lo, y), seq: 16 (over x_hi, z, core).
Axes of the slice: x: 4 (x_hi: 2, x_lo: 2; x = x_hi * 2 + x_lo), y: 4, z: 4, core: 2. Of those that a mesh axis runs over, the one named last changes fastest.
Arguments:
- query_tok: bfloat16 [8, 2048, 2560], P('dp', 'seq'), may hold values from -6 to 6
- key_tok: bfloat16 [8, 2048, 2560], P('dp', 'seq'), may hold values from -6 to 6
- value_tok: bfloat16 [8, 2048, 2560], P('dp', 'seq'), may hold values from -6 to 6
- grad_out: bfloat16 [8, 2048, 5120], P('dp', 'seq'), may hold values from -6 to 6
- out_weight: bfloat16 [32, 128, 5120], P('seq', None, 'dp'), may hold values from -0.125 to 0.125
- block_mask: int32 [20, 16, 16], replicated, may hold values from 0 to 1, as said below
- head_owner: int32 [20], replicated, may hold values from 0 to 15, as said below
Outputs:
- attn_out: bfloat16 [8, 2048, 2560], P('dp', 'seq')
- query_grad: bfloat16 [8, 2048, 2560], P('dp', 'seq')
- key_grad: bfloat16 [8, 2048, 2560], P('dp', 'seq')
- value_grad: bfloat16 [8, 2048, 2560], P('dp', 'seq')
- weight_grad: float32 [32, 128, 5120], P('seq', None, 'dp')
The draws below stay inside these ranges and needn't reach their ends.
Inputs may be any that keep to these rules, and one draw needn't show every extreme that they name: `block_mask`: every diagonal tile is 1; each head has its own share of other tiles. `head_owner`: each value is an index of seq; no index holds more than 2 heads, and some index holds exactly 2.
All inputs are finite; a program needn't handle non-finite values.
Results may differ from the reference program's by a relative error of at most 0.017.
Values may be sent and summed in bfloat16 or wider, within the bound.
No kernel may reach another device: no remote copies, remote signals or barrier semaphores. Data moves between devices by JAX's collectives and lax.ppermute only.
A program may use at most 128 MiB of HBM per device.

```python
import jax
import jax.numpy as jnp
from jax import lax

D = 5120
HEADS = 20
HDIM = 128
HD = 2560
BLOCK = 128
TOKENS = 2048
CLIPS = 8
MOST = 2
SLOTS = 32
NB = 16


def paired_draw(key):
    shape = (CLIPS, TOKENS, HD)
    queries = jnp.clip(jax.random.normal(jax.random.fold_in(key, 11), shape), -6.0, 6.0)
    keys_all = jnp.clip(jax.random.normal(jax.random.fold_in(key, 12), shape), -6.0, 6.0)
    return (queries, keys_all)


def draw_query_tok(key, part):
    return paired_draw(key)[0].astype(jnp.bfloat16)


def draw_key_tok(key, part):
    return paired_draw(key)[1].astype(jnp.bfloat16)


def draw_block_mask(key, part):
    density = jax.random.randint(jax.random.fold_in(key, 31), (HEADS, 1, 1), 100, 251)
    levels = jax.random.randint(jax.random.fold_in(key, 32), (HEADS, NB, NB), 0, 1000)
    diagonal = jnp.arange(NB)[:, None] == jnp.arange(NB)[None, :]
    kept = jnp.logical_or(levels < density, diagonal[None, :, :])
    return jnp.where(kept, 1, 0).astype(jnp.int32)


def draw_head_owner(key, part):
    order = jax.random.permutation(jax.random.fold_in(key, 41), SLOTS)
    return (order[:HEADS] // MOST).astype(jnp.int32)


def block_levels(own_key, shape, shards, smallest, top_value):
    level, own = 1.0, jax.random.fold_in(own_key, 6)
    for dim, parts in shards:
        steps = jnp.exp(jax.random.uniform(jax.random.fold_in(own, dim), (parts,), jnp.float32, smallest / len(shards), top_value / len(shards)))
        level = level * jnp.repeat(steps, shape[dim] // parts).reshape([-1 if axis == dim else 1 for axis in range(len(shape))])
    return level


def centred(stream_key, extent, spread, reach, cuts=(), kind=jnp.bfloat16):
    factor_of = block_levels(stream_key, extent, cuts, -0.22, 0.18) if cuts else 1.0
    result = jax.random.normal(stream_key, extent, jnp.float32) * spread * factor_of
    return jnp.minimum(jnp.maximum(result, -reach), reach).astype(kind)


def setup_inputs(seed: int = 0) -> dict:
    key_of = jax.random.split(jax.random.key(seed), 8)
    query_tok = draw_query_tok(jax.random.fold_in(key_of[7], 71), 0)
    key_tok = draw_key_tok(jax.random.fold_in(key_of[7], 71), 0)
    value_tok = centred(key_of[2], (CLIPS, TOKENS, HD), 1.0, 6.0, ((0, 8), (1, 16)))
    grad_out = centred(key_of[3], (CLIPS, TOKENS, D), 1.0, 6.0, ((0, 8), (1, 16)))
    out_weight = centred(key_of[4], (SLOTS, HDIM, D), HD ** -0.5, 0.125, ((0, 16), (2, 8)))
    block_mask = draw_block_mask(jax.random.fold_in(key_of[7], 71), 0)
    head_owner = draw_head_owner(jax.random.fold_in(key_of[7], 71), 0)
    return {"query_tok": query_tok, "key_tok": key_tok, "value_tok": value_tok, "grad_out": grad_out, "out_weight": out_weight, "block_mask": block_mask, "head_owner": head_owner}


def slot_index(head_owner):
    same_owner = head_owner[:, None] == head_owner[None, :]
    earlier = jnp.arange(HEADS)[None, :] < jnp.arange(HEADS)[:, None]
    owner_rank = jnp.sum(jnp.logical_and(same_owner, earlier), axis=1).astype(jnp.int32)
    return (head_owner * MOST + owner_rank).astype(jnp.int32)


def one_head(queries, keys_all, values_all, cotangent, weight_rows, tiles):
    score_scale = HDIM ** -0.5
    scores = jnp.dot(queries, keys_all.T, preferred_element_type=jnp.float32) * score_scale
    allowed = jnp.repeat(jnp.repeat(tiles, BLOCK, axis=0), BLOCK, axis=1) > 0
    scores = jnp.where(allowed, scores, -jnp.inf)
    row_max = jnp.max(scores, axis=1, keepdims=True)
    expd = jnp.exp(scores - row_max)
    attn_prob = expd / jnp.sum(expd, axis=1, keepdims=True)
    prob_low = attn_prob.astype(jnp.bfloat16)
    attn_out = jnp.dot(prob_low, values_all, preferred_element_type=jnp.float32).astype(jnp.bfloat16)
    grad_attn = jnp.dot(cotangent, weight_rows.T, preferred_element_type=jnp.float32).astype(jnp.bfloat16)
    weight_part = jnp.dot(attn_out.T, cotangent, preferred_element_type=jnp.float32)
    value_grad = jnp.dot(prob_low.T, grad_attn, preferred_element_type=jnp.float32).astype(jnp.bfloat16)
    prob_grad = jnp.dot(grad_attn, values_all.T, preferred_element_type=jnp.float32)
    row_delta = jnp.sum(grad_attn.astype(jnp.float32) * attn_out.astype(jnp.float32), axis=1, keepdims=True)
    score_grad = (attn_prob * (prob_grad - row_delta) * score_scale).astype(jnp.bfloat16)
    query_grad = jnp.dot(score_grad, keys_all, preferred_element_type=jnp.float32).astype(jnp.bfloat16)
    key_grad = jnp.dot(score_grad.T, queries, preferred_element_type=jnp.float32).astype(jnp.bfloat16)
    return attn_out, query_grad, key_grad, value_grad, weight_part


def reference(query_tok, key_tok, value_tok, grad_out, out_weight, block_mask, head_owner):
    slots = slot_index(head_owner)
    head_rows = jnp.take(out_weight, slots, axis=0)

    def by_head(tensor):
        return jnp.transpose(tensor.reshape(CLIPS, TOKENS, HEADS, HDIM), (2, 0, 1, 3))

    q_heads = by_head(query_tok)
    k_heads = by_head(key_tok)
    v_heads = by_head(value_tok)

    def head_work(packed):
        queries, keys_all, values_all, weight_rows, tiles = packed

        def clip_work(inner):
            return one_head(inner[0], inner[1], inner[2], inner[3], weight_rows, tiles)

        outs_all = lax.map(clip_work, (queries, keys_all, values_all, grad_out))
        weight_sum = jnp.sum(outs_all[4], axis=0) * ((CLIPS * TOKENS) ** -0.5)
        return outs_all[0], outs_all[1], outs_all[2], outs_all[3], weight_sum

    results = lax.map(head_work, (q_heads, k_heads, v_heads, head_rows, block_mask))

    def by_token(tensor):
        return jnp.transpose(tensor, (1, 2, 0, 3)).reshape(CLIPS, TOKENS, HD)

    weight_grad = jnp.zeros((SLOTS, HDIM, D), jnp.float32).at[slots].set(results[4])
    return by_token(results[0]), by_token(results[1]), by_token(results[2]), by_token(results[3]), weight_grad
```

```python
import jax
import jax.numpy as jnp
from jax import lax
from jax.sharding import PartitionSpec as P


def slot_table(head_owner, most_slots, seq_count):
    head_count = head_owner.shape[0]
    same_owner = head_owner[:, None] == head_owner[None, :]
    earlier = jnp.arange(head_count)[None, :] < jnp.arange(head_count)[:, None]
    owner_rank = jnp.sum(jnp.logical_and(same_owner, earlier), axis=1)
    slot_index = head_owner * most_slots + owner_rank
    return slot_index[:, None] == jnp.arange(seq_count * most_slots, dtype=jnp.int32)[None, :]


def allowed_rows(blocks, row_first, rows_count, block_len):
    band = lax.dynamic_slice_in_dim(blocks, row_first // block_len, rows_count // block_len, 0)
    spread = jnp.repeat(jnp.repeat(band, block_len, axis=0), block_len, axis=1)
    return spread > 0.5


def block_probs(q_rows, keys_all, allowed, score_scale):
    scores = jnp.dot(q_rows, keys_all.T, preferred_element_type=jnp.float32) * score_scale
    scores = jnp.where(allowed, scores, -jnp.inf)
    row_max = jnp.max(scores, axis=1, keepdims=True)
    expd = jnp.exp(scores - row_max)
    return expd / jnp.sum(expd, axis=1, keepdims=True)


def forward_slot(queries, keys_all, values_all, blocks, rows_count, block_len, score_scale):

    def forward_one_block(number):
        row_first = number * rows_count
        q_rows = lax.dynamic_slice_in_dim(queries, row_first, rows_count, 0)
        attn_prob = block_probs(
            q_rows, keys_all, allowed_rows(blocks, row_first, rows_count, block_len), score_scale
        )
        return jnp.dot(
            attn_prob.astype(jnp.bfloat16), values_all, preferred_element_type=jnp.float32
        ).astype(jnp.bfloat16)

    numbers = jnp.arange(queries.shape[0] // rows_count, dtype=jnp.int32)
    return lax.map(forward_one_block, numbers).reshape(queries.shape)


def backward_slot(
    queries, keys_all, values_all, outputs, grad_attn, blocks, rows_count, block_len, score_scale
):

    def backward_one_block(totals, number):
        key_total, value_total = totals
        row_first = number * rows_count
        q_rows = lax.dynamic_slice_in_dim(queries, row_first, rows_count, 0)
        attn_prob = block_probs(
            q_rows, keys_all, allowed_rows(blocks, row_first, rows_count, block_len), score_scale
        )
        prob_low = attn_prob.astype(jnp.bfloat16)
        grad_rows = lax.dynamic_slice_in_dim(grad_attn, row_first, rows_count, 0)
        out_rows = lax.dynamic_slice_in_dim(outputs, row_first, rows_count, 0)
        value_total = value_total + jnp.dot(
            prob_low.T, grad_rows, preferred_element_type=jnp.float32
        )
        prob_grad = jnp.dot(grad_rows, values_all.T, preferred_element_type=jnp.float32)
        row_delta = jnp.sum(
            grad_rows.astype(jnp.float32) * out_rows.astype(jnp.float32), axis=1, keepdims=True
        )
        score_grad = (attn_prob * (prob_grad - row_delta) * score_scale).astype(jnp.bfloat16)
        query_rows = jnp.dot(score_grad, keys_all, preferred_element_type=jnp.float32).astype(
            jnp.bfloat16
        )
        key_total = key_total + jnp.dot(score_grad.T, q_rows, preferred_element_type=jnp.float32)
        return ((key_total, value_total), query_rows)

    empty = jnp.zeros(queries.shape, jnp.float32)
    numbers = jnp.arange(queries.shape[0] // rows_count, dtype=jnp.int32)
    totals, query_parts = lax.scan(backward_one_block, (empty, empty), numbers)
    query_grad = query_parts.reshape(queries.shape)
    return (query_grad, totals[0].astype(jnp.bfloat16), totals[1].astype(jnp.bfloat16))


def heads_to_tokens(received, select, token_count, head_count, head_dim):
    merged = jnp.einsum("jtd,hj->thd", received[:, 0], select, preferred_element_type=jnp.float32)
    return merged.astype(jnp.bfloat16).reshape(1, token_count, head_count * head_dim)


SEQ = ("chip", "core")


def on_device(query_tok, key_tok, value_tok, grad_out, out_weight, block_mask, head_owner):
    seq_count = lax.axis_size(SEQ)
    most_slots = out_weight.shape[0]
    head_dim = out_weight.shape[1]
    token_count = query_tok.shape[1]
    head_count = block_mask.shape[0]
    length = seq_count * token_count
    block_len = length // block_mask.shape[1]
    rows_count = min(512, length)
    score_scale = head_dim ** (-0.5)
    grad_scale = (lax.axis_size("dp") * length) ** (-0.5)
    table = slot_table(head_owner, most_slots, seq_count)
    select = table.astype(jnp.bfloat16)
    my_first = lax.axis_index(SEQ) * most_slots
    local_select = lax.dynamic_slice_in_dim(table.astype(jnp.float32), my_first, most_slots, 1)
    slot_blocks = jnp.einsum("hs,hab->sab", local_select, block_mask.astype(jnp.float32))
    slot_used = jnp.sum(local_select, axis=0)
    slot_blocks = slot_blocks + (1.0 - slot_used)[:, None, None]

    def to_slots(tensor):
        split_heads = tensor[0].reshape(token_count, head_count, head_dim)
        spread = jnp.einsum("thd,hj->jtd", split_heads, select, preferred_element_type=jnp.float32)
        return spread.astype(jnp.bfloat16).reshape(seq_count, most_slots, token_count, head_dim)

    stacked = jnp.stack([to_slots(query_tok), to_slots(key_tok), to_slots(value_tok)], axis=1)
    arrived = lax.all_to_all(stacked, SEQ, split_axis=0, concat_axis=3, tiled=True)[0]
    slot_query = arrived[0]
    slot_key = arrived[1]
    slot_value = arrived[2]
    weight_full = lax.all_gather(out_weight, "dp", axis=2, tiled=True)
    forward_list = []
    for slot_number in range(most_slots):
        forward_list.append(
            forward_slot(
                slot_query[slot_number],
                slot_key[slot_number],
                slot_value[slot_number],
                slot_blocks[slot_number],
                rows_count,
                block_len,
                score_scale,
            )
        )
    slot_out = jnp.stack(forward_list)

    def back_layout(stacked):
        return stacked.reshape(most_slots, seq_count, token_count, head_dim)

    by_chip = lax.all_gather(grad_out[0], "chip", axis=0, tiled=False)
    dy_rows = lax.all_gather(by_chip, "core", axis=1, tiled=False).reshape(length, grad_out.shape[2])
    part = jnp.einsum(
        "td,shd->sth", dy_rows, weight_full, preferred_element_type=jnp.float32
    ).astype(jnp.bfloat16)
    grad_attn = part
    weight_total = jnp.einsum("sth,td->shd", slot_out, dy_rows, preferred_element_type=jnp.float32)
    grad_attn, weight_total = (grad_attn, weight_total)
    weight_grad = lax.psum_scatter(
        (weight_total * grad_scale).astype(jnp.bfloat16), "dp", scatter_dimension=2, tiled=True
    ).astype(jnp.float32)
    query_list = []
    key_list = []
    value_list = []
    for slot_number in range(most_slots):
        grads = backward_slot(
            slot_query[slot_number],
            slot_key[slot_number],
            slot_value[slot_number],
            slot_out[slot_number],
            grad_attn[slot_number],
            slot_blocks[slot_number],
            rows_count,
            block_len,
            score_scale,
        )
        query_list.append(grads[0])
        key_list.append(grads[1])
        value_list.append(grads[2])
    slot_qgrad = jnp.stack(query_list)
    slot_kgrad = jnp.stack(key_list)
    slot_vgrad = jnp.stack(value_list)
    back_stack = jnp.stack(
        [back_layout(slot_out), back_layout(slot_qgrad), back_layout(slot_kgrad), back_layout(slot_vgrad)]
    )
    all_back = lax.all_to_all(back_stack, SEQ, split_axis=2, concat_axis=1, tiled=True)
    attn_out = heads_to_tokens(all_back[0], select, token_count, head_count, head_dim)
    query_grad = heads_to_tokens(all_back[1], select, token_count, head_count, head_dim)
    key_grad = heads_to_tokens(all_back[2], select, token_count, head_count, head_dim)
    value_grad = heads_to_tokens(all_back[3], select, token_count, head_count, head_dim)
    return (attn_out, query_grad, key_grad, value_grad, weight_grad)


def solution(mesh):
    mesh = jax.sharding.Mesh(
        mesh.devices.reshape(mesh.devices.shape[0], -1, 2), ("dp", "chip", "core")
    )
    placed = (
        P("dp", SEQ, None),
        P("dp", SEQ, None),
        P("dp", SEQ, None),
        P("dp", SEQ, None),
        P(SEQ, None, "dp"),
        P(),
        P(),
    )
    return jax.shard_map(
        on_device,
        mesh=mesh,
        in_specs=placed,
        out_specs=(
            P("dp", SEQ, None),
            P("dp", SEQ, None),
            P("dp", SEQ, None),
            P("dp", SEQ, None),
            P(SEQ, None, "dp"),
        ),
        check_vma=False,
    )
```

```python
import jax
import jax.numpy as jnp
from jax import lax
from jax.sharding import PartitionSpec as P
import functools
from jax.experimental import pallas as pl
from jax.experimental.pallas import tpu as pltpu


TILE = 128


def _scores_pass(mask_ref, s, qi, q, k_ref, s_scr, m_scr, l_scr, nb, scale):
    m_scr[...] = jnp.full(m_scr.shape, -jnp.inf, jnp.float32)
    l_scr[...] = jnp.zeros(l_scr.shape, jnp.float32)

    def first(j, carry):
        @pl.when(mask_ref[s, qi, j] != 0)
        def _():
            col = pl.multiple_of(j * TILE, TILE)
            kj = k_ref[0, pl.ds(col, TILE), :]
            sc = lax.dot_general(q, kj, ((( 1,), (1,)), ((), ())), preferred_element_type=jnp.float32) * scale
            s_scr[:, pl.ds(col, TILE)] = sc
            m_scr[...] = jnp.maximum(m_scr[...], jnp.max(sc, axis=1, keepdims=True))
        return carry

    lax.fori_loop(0, nb, first, 0)

    def second(j, carry):
        @pl.when(mask_ref[s, qi, j] != 0)
        def _():
            col = pl.multiple_of(j * TILE, TILE)
            e = jnp.exp(s_scr[:, pl.ds(col, TILE)] - m_scr[...])
            s_scr[:, pl.ds(col, TILE)] = e
            l_scr[...] = l_scr[...] + jnp.sum(e, axis=1, keepdims=True)
        return carry

    lax.fori_loop(0, nb, second, 0)


def _fwd_kernel(mask_ref, q_ref, k_ref, v_ref, o_ref, s_scr, m_scr, l_scr, acc_scr, *, nb, scale):
    s = pl.program_id(0)
    qi = pl.program_id(1)
    q = q_ref[0]
    _scores_pass(mask_ref, s, qi, q, k_ref, s_scr, m_scr, l_scr, nb, scale)
    acc_scr[...] = jnp.zeros(acc_scr.shape, jnp.float32)

    def third(j, carry):
        @pl.when(mask_ref[s, qi, j] != 0)
        def _():
            col = pl.multiple_of(j * TILE, TILE)
            prob = (s_scr[:, pl.ds(col, TILE)] / l_scr[...]).astype(jnp.bfloat16)
            vj = v_ref[0, pl.ds(col, TILE), :]
            acc_scr[...] += jnp.dot(prob, vj, preferred_element_type=jnp.float32)
        return carry

    lax.fori_loop(0, nb, third, 0)
    o_ref[0] = acc_scr[...].astype(o_ref.dtype)


def _bwd_kernel(mask_ref, q_ref, k_ref, v_ref, o_ref, do_ref, dq_ref, dk_ref, dv_ref,
                s_scr, m_scr, l_scr, dq_scr, dk_scr, dv_scr, *, nb, scale):
    s = pl.program_id(0)
    qi = pl.program_id(1)

    @pl.when(qi == 0)
    def _():
        dk_scr[...] = jnp.zeros(dk_scr.shape, jnp.float32)
        dv_scr[...] = jnp.zeros(dv_scr.shape, jnp.float32)

    q = q_ref[0]
    _scores_pass(mask_ref, s, qi, q, k_ref, s_scr, m_scr, l_scr, nb, scale)
    do = do_ref[0]
    delta = jnp.sum(do.astype(jnp.float32) * o_ref[0].astype(jnp.float32), axis=1, keepdims=True)
    m_scr[...] = delta
    dq_scr[...] = jnp.zeros(dq_scr.shape, jnp.float32)

    def third(j, carry):
        @pl.when(mask_ref[s, qi, j] != 0)
        def _():
            col = pl.multiple_of(j * TILE, TILE)
            prob = s_scr[:, pl.ds(col, TILE)] / l_scr[...]
            low = prob.astype(jnp.bfloat16)
            vj = v_ref[0, pl.ds(col, TILE), :]
            kj = k_ref[0, pl.ds(col, TILE), :]
            dv_scr[pl.ds(col, TILE), :] += lax.dot_general(
                low, do, (((0,), (0,)), ((), ())), preferred_element_type=jnp.float32)
            dp = lax.dot_general(do, vj, (((1,), (1,)), ((), ())), preferred_element_type=jnp.float32)
            ds = (prob * (dp - m_scr[...]) * scale).astype(jnp.bfloat16)
            dq_scr[...] += jnp.dot(ds, kj, preferred_element_type=jnp.float32)
            dk_scr[pl.ds(col, TILE), :] += lax.dot_general(
                ds, q, (((0,), (0,)), ((), ())), preferred_element_type=jnp.float32)
        return carry

    lax.fori_loop(0, nb, third, 0)
    dq_ref[0] = dq_scr[...].astype(dq_ref.dtype)

    @pl.when(qi == nb - 1)
    def _():
        dk_ref[0] = dk_scr[...].astype(dk_ref.dtype)
        dv_ref[0] = dv_scr[...].astype(dv_ref.dtype)


def attn_forward(mask, q, k, v, scale, interpret=False):
    slots, length, hd = q.shape
    nb = length // TILE
    row = pl.BlockSpec((1, TILE, hd), lambda s, i, m: (s, i, 0))
    full = pl.BlockSpec((1, length, hd), lambda s, i, m: (s, 0, 0))
    return pl.pallas_call(
        functools.partial(_fwd_kernel, nb=nb, scale=scale),
        grid_spec=pltpu.PrefetchScalarGridSpec(
            num_scalar_prefetch=1,
            grid=(slots, nb),
            in_specs=[row, full, full],
            out_specs=row,
            scratch_shapes=[
                pltpu.VMEM((TILE, length), jnp.float32),
                pltpu.VMEM((TILE, 1), jnp.float32),
                pltpu.VMEM((TILE, 1), jnp.float32),
                pltpu.VMEM((TILE, hd), jnp.float32),
            ],
        ),
        out_shape=jax.ShapeDtypeStruct(q.shape, jnp.bfloat16),
        compiler_params=pltpu.CompilerParams(dimension_semantics=("arbitrary", "arbitrary")),
        interpret=interpret,
    )(mask, q, k, v)


def attn_backward(mask, q, k, v, o, do, scale, interpret=False):
    slots, length, hd = q.shape
    nb = length // TILE
    row = pl.BlockSpec((1, TILE, hd), lambda s, i, m: (s, i, 0))
    full = pl.BlockSpec((1, length, hd), lambda s, i, m: (s, 0, 0))
    shape = jax.ShapeDtypeStruct(q.shape, jnp.bfloat16)
    return pl.pallas_call(
        functools.partial(_bwd_kernel, nb=nb, scale=scale),
        grid_spec=pltpu.PrefetchScalarGridSpec(
            num_scalar_prefetch=1,
            grid=(slots, nb),
            in_specs=[row, full, full, row, row],
            out_specs=[row, full, full],
            scratch_shapes=[
                pltpu.VMEM((TILE, length), jnp.float32),
                pltpu.VMEM((TILE, 1), jnp.float32),
                pltpu.VMEM((TILE, 1), jnp.float32),
                pltpu.VMEM((TILE, hd), jnp.float32),
                pltpu.VMEM((length, hd), jnp.float32),
                pltpu.VMEM((length, hd), jnp.float32),
            ],
        ),
        out_shape=(shape, shape, shape),
        compiler_params=pltpu.CompilerParams(dimension_semantics=("arbitrary", "arbitrary")),
        interpret=interpret,
    )(mask, q, k, v, o, do)


def slot_table(head_owner, most_slots, seq_count):
    head_count = head_owner.shape[0]
    same_owner = head_owner[:, None] == head_owner[None, :]
    earlier = jnp.arange(head_count)[None, :] < jnp.arange(head_count)[:, None]
    owner_rank = jnp.sum(jnp.logical_and(same_owner, earlier), axis=1)
    slot_index = head_owner * most_slots + owner_rank
    return slot_index[:, None] == jnp.arange(seq_count * most_slots, dtype=jnp.int32)[None, :]


def heads_to_tokens(received, select, token_count, head_count, head_dim):
    merged = jnp.einsum("jtd,hj->thd", received[:, 0], select, preferred_element_type=jnp.float32)
    return merged.astype(jnp.bfloat16).reshape(1, token_count, head_count * head_dim)


def on_device(query_tok, key_tok, value_tok, grad_out, out_weight, block_mask, head_owner):
    seq_count = lax.axis_size("seq")
    most_slots = out_weight.shape[0]
    head_dim = out_weight.shape[1]
    token_count = query_tok.shape[1]
    head_count = block_mask.shape[0]
    length = seq_count * token_count
    score_scale = head_dim ** (-0.5)
    grad_scale = (lax.axis_size("dp") * length) ** (-0.5)
    table = slot_table(head_owner, most_slots, seq_count)
    select = table.astype(jnp.bfloat16)
    my_first = lax.axis_index("seq") * most_slots
    local_select = lax.dynamic_slice_in_dim(table.astype(jnp.float32), my_first, most_slots, 1)
    slot_blocks = jnp.einsum("hs,hab->sab", local_select, block_mask.astype(jnp.float32))
    slot_used = jnp.sum(local_select, axis=0)
    diagonal = jnp.eye(block_mask.shape[1], dtype=jnp.float32)
    slot_blocks = slot_blocks + (1.0 - slot_used)[:, None, None] * diagonal[None]
    slot_mask = (slot_blocks > 0.5).astype(jnp.int32)

    def to_slots(tensor):
        split_heads = tensor[0].reshape(token_count, head_count, head_dim)
        spread = jnp.einsum("thd,hj->jtd", split_heads, select, preferred_element_type=jnp.float32)
        return spread.astype(jnp.bfloat16).reshape(seq_count, most_slots, token_count, head_dim)

    stacked = jnp.stack([to_slots(query_tok), to_slots(key_tok), to_slots(value_tok)], axis=1)
    arrived = lax.all_to_all(stacked, "seq", split_axis=0, concat_axis=3, tiled=True)[0]
    slot_query = arrived[0]
    slot_key = arrived[1]
    slot_value = arrived[2]
    weight_full = lax.all_gather(out_weight, "dp", axis=2, tiled=True)
    slot_out = attn_forward(slot_mask, slot_query, slot_key, slot_value, score_scale)

    def back_layout(stacked):
        return stacked.reshape(most_slots, seq_count, token_count, head_dim)

    out_back = lax.all_to_all(back_layout(slot_out), "seq", split_axis=1, concat_axis=0, tiled=True)

    dy_rows = lax.all_gather(grad_out, "seq", axis=1, tiled=True)[0]
    part = jnp.einsum(
        "td,shd->sth", dy_rows, weight_full, preferred_element_type=jnp.float32
    ).astype(jnp.bfloat16)
    grad_attn = part
    weight_total = jnp.einsum("sth,td->shd", slot_out, dy_rows, preferred_element_type=jnp.float32)
    grad_attn, weight_total = (grad_attn, weight_total)
    weight_grad = lax.psum_scatter(
        (weight_total * grad_scale).astype(jnp.bfloat16), "dp", scatter_dimension=2, tiled=True
    ).astype(jnp.float32)
    slot_qgrad, slot_kgrad, slot_vgrad = attn_backward(
        slot_mask, slot_query, slot_key, slot_value, slot_out, grad_attn, score_scale
    )
    back_stack = jnp.stack([back_layout(slot_qgrad), back_layout(slot_kgrad), back_layout(slot_vgrad)])
    grads_back = lax.all_to_all(back_stack, "seq", split_axis=2, concat_axis=1, tiled=True)
    all_back = (out_back, grads_back[0], grads_back[1], grads_back[2])
    attn_out = heads_to_tokens(all_back[0], select, token_count, head_count, head_dim)
    query_grad = heads_to_tokens(all_back[1], select, token_count, head_count, head_dim)
    key_grad = heads_to_tokens(all_back[2], select, token_count, head_count, head_dim)
    value_grad = heads_to_tokens(all_back[3], select, token_count, head_count, head_dim)
    return (attn_out, query_grad, key_grad, value_grad, weight_grad)


def solution(mesh):
    placed = (
        P("dp", "seq", None),
        P("dp", "seq", None),
        P("dp", "seq", None),
        P("dp", "seq", None),
        P("seq", None, "dp"),
        P(),
        P(),
    )
    return jax.shard_map(
        on_device,
        mesh=mesh,
        in_specs=placed,
        out_specs=(
            P("dp", "seq", None),
            P("dp", "seq", None),
            P("dp", "seq", None),
            P("dp", "seq", None),
            P("seq", None, "dp"),
        ),
        check_vma=False,
    )
```

```python
import jax
import jax.numpy as jnp
from jax import lax
from jax.sharding import PartitionSpec as P
import functools
from jax.experimental import pallas as pl
from jax.experimental.pallas import tpu as pltpu


TILE = 128
NT = (((1,), (1,)), ((), ()))
TN = (((0,), (0,)), ((), ()))


def _probs(q, k, bias, scale):
    sc = lax.dot_general(q, k, NT, preferred_element_type=jnp.float32) * scale + bias
    e = jnp.exp(sc - jnp.max(sc, axis=1, keepdims=True))
    return e / jnp.sum(e, axis=1, keepdims=True)


def _fwd_kernel(q_ref, k_ref, v_ref, b_ref, o_ref, *, scale):
    prob = _probs(q_ref[0], k_ref[0], b_ref[0, 0], scale)
    out = jnp.dot(prob.astype(jnp.bfloat16), v_ref[0], preferred_element_type=jnp.float32)
    o_ref[0] = out.astype(o_ref.dtype)


def _bwd_kernel(q_ref, k_ref, v_ref, b_ref, o_ref, do_ref, dq_ref, dk_ref, dv_ref,
                dk_scr, dv_scr, *, nb, scale):
    qi = pl.program_id(1)

    @pl.when(qi == 0)
    def _():
        dk_scr[...] = jnp.zeros(dk_scr.shape, jnp.float32)
        dv_scr[...] = jnp.zeros(dv_scr.shape, jnp.float32)

    q = q_ref[0]
    k = k_ref[0]
    v = v_ref[0]
    do = do_ref[0]
    prob = _probs(q, k, b_ref[0, 0], scale)
    low = prob.astype(jnp.bfloat16)
    delta = jnp.sum(do.astype(jnp.float32) * o_ref[0].astype(jnp.float32), axis=1, keepdims=True)
    dv_scr[...] += lax.dot_general(low, do, TN, preferred_element_type=jnp.float32)
    dp = lax.dot_general(do, v, NT, preferred_element_type=jnp.float32)
    ds = (prob * (dp - delta) * scale).astype(jnp.bfloat16)
    dq_ref[0] = jnp.dot(ds, k, preferred_element_type=jnp.float32).astype(dq_ref.dtype)
    dk_scr[...] += lax.dot_general(ds, q, TN, preferred_element_type=jnp.float32)

    @pl.when(qi == nb - 1)
    def _():
        dk_ref[0] = dk_scr[...].astype(dk_ref.dtype)
        dv_ref[0] = dv_scr[...].astype(dv_ref.dtype)


def mask_bias(slot_mask, length):
    spread = jnp.repeat(slot_mask, length // slot_mask.shape[2], axis=2)
    return jnp.where(spread > 0, 0.0, -jnp.inf).astype(jnp.float32)[:, :, None, :]


def attn_forward(bias, q, k, v, scale, interpret=False):
    slots, length, hd = q.shape
    nb = length // TILE
    row = pl.BlockSpec((1, TILE, hd), lambda s, i: (s, i, 0))
    full = pl.BlockSpec((1, length, hd), lambda s, i: (s, 0, 0))
    brow = pl.BlockSpec((1, 1, 1, length), lambda s, i: (s, i, 0, 0))
    return pl.pallas_call(
        functools.partial(_fwd_kernel, scale=scale),
        grid=(slots, nb),
        in_specs=[row, full, full, brow],
        out_specs=row,
        out_shape=jax.ShapeDtypeStruct(q.shape, jnp.bfloat16),
        compiler_params=pltpu.CompilerParams(dimension_semantics=("arbitrary", "arbitrary")),
        interpret=interpret,
    )(q, k, v, bias)


def attn_backward(bias, q, k, v, o, do, scale, interpret=False):
    slots, length, hd = q.shape
    nb = length // TILE
    row = pl.BlockSpec((1, TILE, hd), lambda s, i: (s, i, 0))
    full = pl.BlockSpec((1, length, hd), lambda s, i: (s, 0, 0))
    brow = pl.BlockSpec((1, 1, 1, length), lambda s, i: (s, i, 0, 0))
    shape = jax.ShapeDtypeStruct(q.shape, jnp.bfloat16)
    return pl.pallas_call(
        functools.partial(_bwd_kernel, nb=nb, scale=scale),
        grid=(slots, nb),
        in_specs=[row, full, full, brow, row, row],
        out_specs=[row, full, full],
        out_shape=(shape, shape, shape),
        scratch_shapes=[pltpu.VMEM((length, hd), jnp.float32), pltpu.VMEM((length, hd), jnp.float32)],
        compiler_params=pltpu.CompilerParams(dimension_semantics=("arbitrary", "arbitrary")),
        interpret=interpret,
    )(q, k, v, bias, o, do)


def slot_table(head_owner, most_slots, seq_count):
    head_count = head_owner.shape[0]
    same_owner = head_owner[:, None] == head_owner[None, :]
    earlier = jnp.arange(head_count)[None, :] < jnp.arange(head_count)[:, None]
    owner_rank = jnp.sum(jnp.logical_and(same_owner, earlier), axis=1)
    slot_index = head_owner * most_slots + owner_rank
    return slot_index[:, None] == jnp.arange(seq_count * most_slots, dtype=jnp.int32)[None, :]


def heads_to_tokens(received, select, token_count, head_count, head_dim):
    merged = jnp.einsum("jtd,hj->thd", received[:, 0], select, preferred_element_type=jnp.float32)
    return merged.astype(jnp.bfloat16).reshape(1, token_count, head_count * head_dim)


def on_device(query_tok, key_tok, value_tok, grad_out, out_weight, block_mask, head_owner):
    seq_count = lax.axis_size("seq")
    most_slots = out_weight.shape[0]
    head_dim = out_weight.shape[1]
    token_count = query_tok.shape[1]
    head_count = block_mask.shape[0]
    length = seq_count * token_count
    score_scale = head_dim ** (-0.5)
    grad_scale = (lax.axis_size("dp") * length) ** (-0.5)
    table = slot_table(head_owner, most_slots, seq_count)
    select = table.astype(jnp.bfloat16)
    my_first = lax.axis_index("seq") * most_slots
    local_select = lax.dynamic_slice_in_dim(table.astype(jnp.float32), my_first, most_slots, 1)
    slot_blocks = jnp.einsum("hs,hab->sab", local_select, block_mask.astype(jnp.float32))
    slot_used = jnp.sum(local_select, axis=0)
    diagonal = jnp.eye(block_mask.shape[1], dtype=jnp.float32)
    slot_blocks = slot_blocks + (1.0 - slot_used)[:, None, None] * diagonal[None]
    slot_mask = (slot_blocks > 0.5).astype(jnp.int32)
    bias = mask_bias(slot_mask, length)

    def to_slots(tensor):
        split_heads = tensor[0].reshape(token_count, head_count, head_dim)
        spread = jnp.einsum("thd,hj->jtd", split_heads, select, preferred_element_type=jnp.float32)
        return spread.astype(jnp.bfloat16).reshape(seq_count, most_slots, token_count, head_dim)

    stacked = jnp.stack([to_slots(query_tok), to_slots(key_tok), to_slots(value_tok)], axis=1)
    arrived = lax.all_to_all(stacked, "seq", split_axis=0, concat_axis=3, tiled=True)[0]
    slot_query = arrived[0]
    slot_key = arrived[1]
    slot_value = arrived[2]
    weight_full = lax.all_gather(out_weight, "dp", axis=2, tiled=True)
    slot_out = attn_forward(bias, slot_query, slot_key, slot_value, score_scale)

    def back_layout(stacked):
        return stacked.reshape(most_slots, seq_count, token_count, head_dim)

    out_back = lax.all_to_all(back_layout(slot_out), "seq", split_axis=1, concat_axis=0, tiled=True)

    dy_rows = lax.all_gather(grad_out, "seq", axis=1, tiled=True)[0]
    part = jnp.einsum(
        "td,shd->sth", dy_rows, weight_full, preferred_element_type=jnp.float32
    ).astype(jnp.bfloat16)
    grad_attn = part
    weight_total = jnp.einsum("sth,td->shd", slot_out, dy_rows, preferred_element_type=jnp.float32)
    grad_attn, weight_total = (grad_attn, weight_total)
    weight_grad = lax.psum_scatter(
        (weight_total * grad_scale).astype(jnp.bfloat16), "dp", scatter_dimension=2, tiled=True
    ).astype(jnp.float32)
    slot_qgrad, slot_kgrad, slot_vgrad = attn_backward(
        bias, slot_query, slot_key, slot_value, slot_out, grad_attn, score_scale
    )
    back_stack = jnp.stack([back_layout(slot_qgrad), back_layout(slot_kgrad), back_layout(slot_vgrad)])
    grads_back = lax.all_to_all(back_stack, "seq", split_axis=2, concat_axis=1, tiled=True)
    all_back = (out_back, grads_back[0], grads_back[1], grads_back[2])
    attn_out = heads_to_tokens(all_back[0], select, token_count, head_count, head_dim)
    query_grad = heads_to_tokens(all_back[1], select, token_count, head_count, head_dim)
    key_grad = heads_to_tokens(all_back[2], select, token_count, head_count, head_dim)
    value_grad = heads_to_tokens(all_back[3], select, token_count, head_count, head_dim)
    return (attn_out, query_grad, key_grad, value_grad, weight_grad)


def solution(mesh):
    placed = (
        P("dp", "seq", None),
        P("dp", "seq", None),
        P("dp", "seq", None),
        P("dp", "seq", None),
        P("seq", None, "dp"),
        P(),
        P(),
    )
    return jax.shard_map(
        on_device,
        mesh=mesh,
        in_specs=placed,
        out_specs=(
            P("dp", "seq", None),
            P("dp", "seq", None),
            P("dp", "seq", None),
            P("dp", "seq", None),
            P("seq", None, "dp"),
        ),
        check_vma=False,
    )
```

```python
import jax
import jax.numpy as jnp
from jax import lax
from jax.sharding import PartitionSpec as P
import functools
from jax.experimental import pallas as pl
from jax.experimental.pallas import tpu as pltpu


TILE = 128
NT = (((1,), (1,)), ((), ()))
TN = (((0,), (0,)), ((), ()))


def _probs(q, k, bias, scale):
    sc = lax.dot_general(q, k, NT, preferred_element_type=jnp.float32) * scale + bias
    e = jnp.exp(sc - jnp.max(sc, axis=1, keepdims=True))
    return e / jnp.sum(e, axis=1, keepdims=True)


def _fwd_kernel(q_ref, k_ref, v_ref, b_ref, o_ref, *, scale):
    prob = _probs(q_ref[0], k_ref[0], b_ref[0, 0], scale)
    out = jnp.dot(prob.astype(jnp.bfloat16), v_ref[0], preferred_element_type=jnp.float32)
    o_ref[0] = out.astype(o_ref.dtype)


def _bwd_kernel(q_ref, k_ref, v_ref, b_ref, o_ref, do_ref, dq_ref, dk_ref, dv_ref,
                dk_scr, dv_scr, *, nb, scale):
    qi = pl.program_id(1)

    @pl.when(qi == 0)
    def _():
        dk_scr[...] = jnp.zeros(dk_scr.shape, jnp.float32)
        dv_scr[...] = jnp.zeros(dv_scr.shape, jnp.float32)

    q = q_ref[0]
    k = k_ref[0]
    v = v_ref[0]
    do = do_ref[0]
    prob = _probs(q, k, b_ref[0, 0], scale)
    low = prob.astype(jnp.bfloat16)
    delta = jnp.sum(do.astype(jnp.float32) * o_ref[0].astype(jnp.float32), axis=1, keepdims=True)
    dv_scr[...] += lax.dot_general(low, do, TN, preferred_element_type=jnp.float32)
    dp = lax.dot_general(do, v, NT, preferred_element_type=jnp.float32)
    ds = (prob * (dp - delta) * scale).astype(jnp.bfloat16)
    dq_ref[0] = jnp.dot(ds, k, preferred_element_type=jnp.float32).astype(dq_ref.dtype)
    dk_scr[...] += lax.dot_general(ds, q, TN, preferred_element_type=jnp.float32)

    @pl.when(qi == nb - 1)
    def _():
        dk_ref[0] = dk_scr[...].astype(dk_ref.dtype)
        dv_ref[0] = dv_scr[...].astype(dv_ref.dtype)


def mask_bias(slot_mask, length):
    spread = jnp.repeat(slot_mask, length // slot_mask.shape[2], axis=2)
    return jnp.where(spread > 0, 0.0, -jnp.inf).astype(jnp.float32)[:, :, None, :]


def attn_forward(bias, q, k, v, scale, interpret=False):
    slots, length, hd = q.shape
    nb = length // TILE
    row = pl.BlockSpec((1, TILE, hd), lambda s, i: (s, i, 0))
    full = pl.BlockSpec((1, length, hd), lambda s, i: (s, 0, 0))
    brow = pl.BlockSpec((1, 1, 1, length), lambda s, i: (s, i, 0, 0))
    return pl.pallas_call(
        functools.partial(_fwd_kernel, scale=scale),
        grid=(slots, nb),
        in_specs=[row, full, full, brow],
        out_specs=row,
        out_shape=jax.ShapeDtypeStruct(q.shape, jnp.bfloat16),
        compiler_params=pltpu.CompilerParams(dimension_semantics=("arbitrary", "arbitrary")),
        interpret=interpret,
    )(q, k, v, bias)


def attn_backward(bias, q, k, v, o, do, scale, interpret=False):
    slots, length, hd = q.shape
    nb = length // TILE
    row = pl.BlockSpec((1, TILE, hd), lambda s, i: (s, i, 0))
    full = pl.BlockSpec((1, length, hd), lambda s, i: (s, 0, 0))
    brow = pl.BlockSpec((1, 1, 1, length), lambda s, i: (s, i, 0, 0))
    shape = jax.ShapeDtypeStruct(q.shape, jnp.bfloat16)
    return pl.pallas_call(
        functools.partial(_bwd_kernel, nb=nb, scale=scale),
        grid=(slots, nb),
        in_specs=[row, full, full, brow, row, row],
        out_specs=[row, full, full],
        out_shape=(shape, shape, shape),
        scratch_shapes=[pltpu.VMEM((length, hd), jnp.float32), pltpu.VMEM((length, hd), jnp.float32)],
        compiler_params=pltpu.CompilerParams(dimension_semantics=("arbitrary", "arbitrary")),
        interpret=interpret,
    )(q, k, v, bias, o, do)


def slot_table(head_owner, most_slots, seq_count):
    head_count = head_owner.shape[0]
    same_owner = head_owner[:, None] == head_owner[None, :]
    earlier = jnp.arange(head_count)[None, :] < jnp.arange(head_count)[:, None]
    owner_rank = jnp.sum(jnp.logical_and(same_owner, earlier), axis=1)
    slot_index = head_owner * most_slots + owner_rank
    return slot_index[:, None] == jnp.arange(seq_count * most_slots, dtype=jnp.int32)[None, :]


def heads_to_tokens(received, select, token_count, head_count, head_dim):
    merged = jnp.einsum("jtd,hj->thd", received[:, 0], select, preferred_element_type=jnp.float32)
    return merged.astype(jnp.bfloat16).reshape(1, token_count, head_count * head_dim)


def on_device(query_tok, key_tok, value_tok, grad_out, out_weight, block_mask, head_owner):
    seq_count = lax.axis_size("seq")
    most_slots = out_weight.shape[0]
    head_dim = out_weight.shape[1]
    token_count = query_tok.shape[1]
    head_count = block_mask.shape[0]
    length = seq_count * token_count
    score_scale = head_dim ** (-0.5)
    grad_scale = (lax.axis_size("dp") * length) ** (-0.5)
    table = slot_table(head_owner, most_slots, seq_count)
    select = table.astype(jnp.bfloat16)
    my_first = lax.axis_index("seq") * most_slots
    local_select = lax.dynamic_slice_in_dim(table.astype(jnp.float32), my_first, most_slots, 1)
    slot_blocks = jnp.einsum("hs,hab->sab", local_select, block_mask.astype(jnp.float32))
    slot_used = jnp.sum(local_select, axis=0)
    diagonal = jnp.eye(block_mask.shape[1], dtype=jnp.float32)
    slot_blocks = slot_blocks + (1.0 - slot_used)[:, None, None] * diagonal[None]
    slot_mask = (slot_blocks > 0.5).astype(jnp.int32)
    bias = mask_bias(slot_mask, length)

    def to_slots(tensor):
        split_heads = tensor[0].reshape(token_count, head_count, head_dim)
        spread = jnp.einsum("thd,hj->jtd", split_heads, select, preferred_element_type=jnp.float32)
        return spread.astype(jnp.bfloat16).reshape(seq_count, most_slots, token_count, head_dim)

    stacked = jnp.stack([to_slots(query_tok), to_slots(key_tok), to_slots(value_tok)], axis=1)
    arrived = lax.all_to_all(stacked, "seq", split_axis=0, concat_axis=3, tiled=True)[0]
    slot_query = arrived[0]
    slot_key = arrived[1]
    slot_value = arrived[2]
    dp_count = lax.axis_size("dp")
    weight_copies = jnp.broadcast_to(out_weight[None], (dp_count,) + out_weight.shape)
    weight_parts = lax.all_to_all(weight_copies, "dp", split_axis=0, concat_axis=0, tiled=True)
    slot_out = attn_forward(bias, slot_query, slot_key, slot_value, score_scale)

    def back_layout(stacked):
        return stacked.reshape(most_slots, seq_count, token_count, head_dim)

    out_back = lax.all_to_all(back_layout(slot_out), "seq", split_axis=1, concat_axis=0, tiled=True)

    dy_rows = lax.all_gather(grad_out, "seq", axis=1, tiled=True)[0]
    part = jnp.einsum(
        "tjd,jshd->sth",
        dy_rows.reshape(length, dp_count, out_weight.shape[2]),
        weight_parts,
        preferred_element_type=jnp.float32,
    ).astype(jnp.bfloat16)
    grad_attn = part
    weight_total = jnp.einsum("sth,td->shd", slot_out, dy_rows, preferred_element_type=jnp.float32)
    grad_attn, weight_total = (grad_attn, weight_total)
    weight_grad = lax.psum_scatter(
        (weight_total * grad_scale).astype(jnp.bfloat16), "dp", scatter_dimension=2, tiled=True
    ).astype(jnp.float32)
    grads_parts = []
    for slot_number in range(most_slots):
        one = slice(slot_number, slot_number + 1)
        slot_grads = attn_backward(
            bias[one],
            slot_query[one],
            slot_key[one],
            slot_value[one],
            slot_out[one],
            grad_attn[one],
            score_scale,
        )
        one_stack = jnp.stack([g.reshape(1, seq_count, token_count, head_dim) for g in slot_grads])
        grads_parts.append(lax.all_to_all(one_stack, "seq", split_axis=2, concat_axis=1, tiled=True))
    grads_back = jnp.stack(grads_parts, axis=2).reshape(3, seq_count * most_slots, 1, token_count, head_dim)
    all_back = (out_back, grads_back[0], grads_back[1], grads_back[2])
    attn_out = heads_to_tokens(all_back[0], select, token_count, head_count, head_dim)
    query_grad = heads_to_tokens(all_back[1], select, token_count, head_count, head_dim)
    key_grad = heads_to_tokens(all_back[2], select, token_count, head_count, head_dim)
    value_grad = heads_to_tokens(all_back[3], select, token_count, head_count, head_dim)
    return (attn_out, query_grad, key_grad, value_grad, weight_grad)


def solution(mesh):
    placed = (
        P("dp", "seq", None),
        P("dp", "seq", None),
        P("dp", "seq", None),
        P("dp", "seq", None),
        P("seq", None, "dp"),
        P(),
        P(),
    )
    return jax.shard_map(
        on_device,
        mesh=mesh,
        in_specs=placed,
        out_specs=(
            P("dp", "seq", None),
            P("dp", "seq", None),
            P("dp", "seq", None),
            P("dp", "seq", None),
            P("seq", None, "dp"),
        ),
        check_vma=False,
    )
```

```python
import jax
import jax.numpy as jnp
from jax import lax
from jax.sharding import PartitionSpec as P
import functools
from jax.experimental import pallas as pl
from jax.experimental.pallas import tpu as pltpu


TILE = 128
NT = (((1,), (1,)), ((), ()))
TN = (((0,), (0,)), ((), ()))


def _probs(q, k, bias, scale):
    sc = lax.dot_general(q, k, NT, preferred_element_type=jnp.float32) * scale + bias
    e = jnp.exp(sc - jnp.max(sc, axis=1, keepdims=True))
    return e / jnp.sum(e, axis=1, keepdims=True)


def _fwd_kernel(q_ref, k_ref, v_ref, b_ref, o_ref, *, scale):
    prob = _probs(q_ref[0], k_ref[0], b_ref[0, 0], scale)
    out = jnp.dot(prob.astype(jnp.bfloat16), v_ref[0], preferred_element_type=jnp.float32)
    o_ref[0] = out.astype(o_ref.dtype)


def _bwd_kernel(q_ref, k_ref, v_ref, b_ref, o_ref, do_ref, dq_ref, dk_ref, dv_ref,
                dk_scr, dv_scr, *, nb, scale):
    qi = pl.program_id(1)

    @pl.when(qi == 0)
    def _():
        dk_scr[...] = jnp.zeros(dk_scr.shape, jnp.float32)
        dv_scr[...] = jnp.zeros(dv_scr.shape, jnp.float32)

    q = q_ref[0]
    k = k_ref[0]
    v = v_ref[0]
    do = do_ref[0]
    prob = _probs(q, k, b_ref[0, 0], scale)
    low = prob.astype(jnp.bfloat16)
    delta = jnp.sum(do.astype(jnp.float32) * o_ref[0].astype(jnp.float32), axis=1, keepdims=True)
    dv_scr[...] += lax.dot_general(low, do, TN, preferred_element_type=jnp.float32)
    dp = lax.dot_general(do, v, NT, preferred_element_type=jnp.float32)
    ds = (prob * (dp - delta) * scale).astype(jnp.bfloat16)
    dq_ref[0] = jnp.dot(ds, k, preferred_element_type=jnp.float32).astype(dq_ref.dtype)
    dk_scr[...] += lax.dot_general(ds, q, TN, preferred_element_type=jnp.float32)

    @pl.when(qi == nb - 1)
    def _():
        dk_ref[0] = dk_scr[...].astype(dk_ref.dtype)
        dv_ref[0] = dv_scr[...].astype(dv_ref.dtype)


def mask_bias(slot_mask, length):
    spread = jnp.repeat(slot_mask, length // slot_mask.shape[2], axis=2)
    return jnp.where(spread > 0, 0.0, -jnp.inf).astype(jnp.float32)[:, :, None, :]


def attn_forward(bias, q, k, v, scale, interpret=False):
    slots, length, hd = q.shape
    nb = length // TILE
    row = pl.BlockSpec((1, TILE, hd), lambda s, i: (s, i, 0))
    full = pl.BlockSpec((1, length, hd), lambda s, i: (s, 0, 0))
    brow = pl.BlockSpec((1, 1, 1, length), lambda s, i: (s, i, 0, 0))
    return pl.pallas_call(
        functools.partial(_fwd_kernel, scale=scale),
        grid=(slots, nb),
        in_specs=[row, full, full, brow],
        out_specs=row,
        out_shape=jax.ShapeDtypeStruct(q.shape, jnp.bfloat16),
        compiler_params=pltpu.CompilerParams(dimension_semantics=("arbitrary", "arbitrary")),
        interpret=interpret,
    )(q, k, v, bias)


def attn_backward(bias, q, k, v, o, do, scale, interpret=False):
    slots, length, hd = q.shape
    nb = length // TILE
    row = pl.BlockSpec((1, TILE, hd), lambda s, i: (s, i, 0))
    full = pl.BlockSpec((1, length, hd), lambda s, i: (s, 0, 0))
    brow = pl.BlockSpec((1, 1, 1, length), lambda s, i: (s, i, 0, 0))
    shape = jax.ShapeDtypeStruct(q.shape, jnp.bfloat16)
    return pl.pallas_call(
        functools.partial(_bwd_kernel, nb=nb, scale=scale),
        grid=(slots, nb),
        in_specs=[row, full, full, brow, row, row],
        out_specs=[row, full, full],
        out_shape=(shape, shape, shape),
        scratch_shapes=[pltpu.VMEM((length, hd), jnp.float32), pltpu.VMEM((length, hd), jnp.float32)],
        compiler_params=pltpu.CompilerParams(dimension_semantics=("arbitrary", "arbitrary")),
        interpret=interpret,
    )(q, k, v, bias, o, do)


def slot_table(head_owner, most_slots, seq_count):
    head_count = head_owner.shape[0]
    same_owner = head_owner[:, None] == head_owner[None, :]
    earlier = jnp.arange(head_count)[None, :] < jnp.arange(head_count)[:, None]
    owner_rank = jnp.sum(jnp.logical_and(same_owner, earlier), axis=1)
    slot_index = head_owner * most_slots + owner_rank
    return slot_index[:, None] == jnp.arange(seq_count * most_slots, dtype=jnp.int32)[None, :]


def heads_to_tokens(received, select, token_count, head_count, head_dim):
    merged = jnp.einsum("jtd,hj->thd", received[:, 0], select, preferred_element_type=jnp.float32)
    return merged.astype(jnp.bfloat16).reshape(1, token_count, head_count * head_dim)


def on_device(query_tok, key_tok, value_tok, grad_out, out_weight, block_mask, head_owner):
    seq_count = lax.axis_size("seq")
    most_slots = out_weight.shape[0]
    head_dim = out_weight.shape[1]
    token_count = query_tok.shape[1]
    head_count = block_mask.shape[0]
    length = seq_count * token_count
    score_scale = head_dim ** (-0.5)
    grad_scale = (lax.axis_size("dp") * length) ** (-0.5)
    table = slot_table(head_owner, most_slots, seq_count)
    select = table.astype(jnp.bfloat16)
    my_first = lax.axis_index("seq") * most_slots
    local_select = lax.dynamic_slice_in_dim(table.astype(jnp.float32), my_first, most_slots, 1)
    slot_blocks = jnp.einsum("hs,hab->sab", local_select, block_mask.astype(jnp.float32))
    slot_used = jnp.sum(local_select, axis=0)
    diagonal = jnp.eye(block_mask.shape[1], dtype=jnp.float32)
    slot_blocks = slot_blocks + (1.0 - slot_used)[:, None, None] * diagonal[None]
    slot_mask = (slot_blocks > 0.5).astype(jnp.int32)
    bias = mask_bias(slot_mask, length)

    def to_slots(tensor):
        split_heads = tensor[0].reshape(token_count, head_count, head_dim)
        spread = jnp.einsum("thd,hj->jtd", split_heads, select, preferred_element_type=jnp.float32)
        return spread.astype(jnp.bfloat16).reshape(seq_count, most_slots, token_count, head_dim)

    stacked = jnp.stack([to_slots(query_tok), to_slots(key_tok), to_slots(value_tok)], axis=1)
    arrived = lax.all_to_all(stacked, "seq", split_axis=0, concat_axis=3, tiled=True)[0]
    slot_query = arrived[0]
    slot_key = arrived[1]
    slot_value = arrived[2]
    dp_count = lax.axis_size("dp")
    weight_copies = jnp.broadcast_to(out_weight[None], (dp_count,) + out_weight.shape)
    weight_parts = lax.all_to_all(weight_copies, "dp", split_axis=0, concat_axis=0, tiled=True)
    slot_out = attn_forward(bias, slot_query, slot_key, slot_value, score_scale)

    def back_layout(stacked):
        return stacked.reshape(most_slots, seq_count, token_count, head_dim)

    out_back = lax.all_to_all(back_layout(slot_out), "seq", split_axis=1, concat_axis=0, tiled=True)

    weight_full = jnp.transpose(weight_parts, (1, 2, 0, 3)).reshape(
        most_slots, head_dim, dp_count * out_weight.shape[2]
    )
    feature_count = grad_out.shape[2]
    sc_features = feature_count - feature_count // 5 // 128 * 128
    dy_first = lax.all_gather(grad_out[0, :, :sc_features], "seq", axis=0, tiled=True)
    dy_copies = jnp.broadcast_to(
        grad_out[:, :, sc_features:], (seq_count, token_count, feature_count - sc_features)
    )
    dy_second = lax.all_to_all(dy_copies, "seq", split_axis=0, concat_axis=0, tiled=True).reshape(
        length, feature_count - sc_features
    )
    part = (
        jnp.einsum(
            "td,shd->sth", dy_first, weight_full[:, :, :sc_features], preferred_element_type=jnp.float32
        )
        + jnp.einsum(
            "td,shd->sth", dy_second, weight_full[:, :, sc_features:], preferred_element_type=jnp.float32
        )
    ).astype(jnp.bfloat16)
    grad_attn = part
    weight_total = jnp.concatenate(
        [
            jnp.einsum("sth,td->shd", slot_out, dy_first, preferred_element_type=jnp.float32),
            jnp.einsum("sth,td->shd", slot_out, dy_second, preferred_element_type=jnp.float32),
        ],
        axis=2,
    )
    grad_attn, weight_total = (grad_attn, weight_total)
    weight_grad = lax.psum_scatter(
        (weight_total * grad_scale).astype(jnp.bfloat16), "dp", scatter_dimension=2, tiled=True
    ).astype(jnp.float32)
    grads_parts = []
    for slot_number in range(most_slots):
        one = slice(slot_number, slot_number + 1)
        slot_grads = attn_backward(
            bias[one],
            slot_query[one],
            slot_key[one],
            slot_value[one],
            slot_out[one],
            grad_attn[one],
            score_scale,
        )
        one_stack = jnp.stack([g.reshape(1, seq_count, token_count, head_dim) for g in slot_grads])
        grads_parts.append(lax.all_to_all(one_stack, "seq", split_axis=2, concat_axis=1, tiled=True))
    grads_back = jnp.stack(grads_parts, axis=2).reshape(3, seq_count * most_slots, 1, token_count, head_dim)
    all_back = (out_back, grads_back[0], grads_back[1], grads_back[2])
    attn_out = heads_to_tokens(all_back[0], select, token_count, head_count, head_dim)
    query_grad = heads_to_tokens(all_back[1], select, token_count, head_count, head_dim)
    key_grad = heads_to_tokens(all_back[2], select, token_count, head_count, head_dim)
    value_grad = heads_to_tokens(all_back[3], select, token_count, head_count, head_dim)
    return (attn_out, query_grad, key_grad, value_grad, weight_grad)


def solution(mesh):
    placed = (
        P("dp", "seq", None),
        P("dp", "seq", None),
        P("dp", "seq", None),
        P("dp", "seq", None),
        P("seq", None, "dp"),
        P(),
        P(),
    )
    return jax.shard_map(
        on_device,
        mesh=mesh,
        in_specs=placed,
        out_specs=(
            P("dp", "seq", None),
            P("dp", "seq", None),
            P("dp", "seq", None),
            P("dp", "seq", None),
            P("seq", None, "dp"),
        ),
        check_vma=False,
    )
```

```python
import jax
import jax.numpy as jnp
from jax import lax
from jax.sharding import PartitionSpec as P
import functools
from jax.experimental import pallas as pl
from jax.experimental.pallas import tpu as pltpu


TILE = 128
NT = (((1,), (1,)), ((), ()))
TN = (((0,), (0,)), ((), ()))


def _probs(q, k, bias, scale):
    sc = lax.dot_general(q, k, NT, preferred_element_type=jnp.float32) * scale + bias
    e = jnp.exp(sc - jnp.max(sc, axis=1, keepdims=True))
    return e / jnp.sum(e, axis=1, keepdims=True)


def _fwd_kernel(q_ref, k_ref, v_ref, b_ref, o_ref, *, scale):
    prob = _probs(q_ref[0], k_ref[0], b_ref[0, 0], scale)
    out = jnp.dot(prob.astype(jnp.bfloat16), v_ref[0], preferred_element_type=jnp.float32)
    o_ref[0] = out.astype(o_ref.dtype)


def _bwd_kernel(q_ref, k_ref, v_ref, b_ref, o_ref, do_ref, dq_ref, dk_ref, dv_ref,
                dk_scr, dv_scr, *, nb, scale):
    qi = pl.program_id(1)

    @pl.when(qi == 0)
    def _():
        dk_scr[...] = jnp.zeros(dk_scr.shape, jnp.float32)
        dv_scr[...] = jnp.zeros(dv_scr.shape, jnp.float32)

    q = q_ref[0]
    k = k_ref[0]
    v = v_ref[0]
    do = do_ref[0]
    prob = _probs(q, k, b_ref[0, 0], scale)
    low = prob.astype(jnp.bfloat16)
    delta = jnp.sum(do.astype(jnp.float32) * o_ref[0].astype(jnp.float32), axis=1, keepdims=True)
    dv_scr[...] += lax.dot_general(low, do, TN, preferred_element_type=jnp.float32)
    dp = lax.dot_general(do, v, NT, preferred_element_type=jnp.float32)
    ds = (prob * (dp - delta) * scale).astype(jnp.bfloat16)
    dq_ref[0] = jnp.dot(ds, k, preferred_element_type=jnp.float32).astype(dq_ref.dtype)
    dk_scr[...] += lax.dot_general(ds, q, TN, preferred_element_type=jnp.float32)

    @pl.when(qi == nb - 1)
    def _():
        dk_ref[0] = dk_scr[...].astype(dk_ref.dtype)
        dv_ref[0] = dv_scr[...].astype(dv_ref.dtype)


def mask_bias(slot_mask, length):
    spread = jnp.repeat(slot_mask, length // slot_mask.shape[2], axis=2)
    return jnp.where(spread > 0, 0.0, -jnp.inf).astype(jnp.float32)[:, :, None, :]


def attn_forward(bias, q, k, v, scale, interpret=False):
    slots, length, hd = q.shape
    nb = length // TILE
    row = pl.BlockSpec((1, TILE, hd), lambda s, i: (s, i, 0))
    full = pl.BlockSpec((1, length, hd), lambda s, i: (s, 0, 0))
    brow = pl.BlockSpec((1, 1, 1, length), lambda s, i: (s, i, 0, 0))
    return pl.pallas_call(
        functools.partial(_fwd_kernel, scale=scale),
        grid=(slots, nb),
        in_specs=[row, full, full, brow],
        out_specs=row,
        out_shape=jax.ShapeDtypeStruct(q.shape, jnp.bfloat16),
        compiler_params=pltpu.CompilerParams(dimension_semantics=("arbitrary", "arbitrary")),
        interpret=interpret,
    )(q, k, v, bias)


def attn_backward(bias, q, k, v, o, do, scale, interpret=False):
    slots, length, hd = q.shape
    nb = length // TILE
    row = pl.BlockSpec((1, TILE, hd), lambda s, i: (s, i, 0))
    full = pl.BlockSpec((1, length, hd), lambda s, i: (s, 0, 0))
    brow = pl.BlockSpec((1, 1, 1, length), lambda s, i: (s, i, 0, 0))
    shape = jax.ShapeDtypeStruct(q.shape, jnp.bfloat16)
    return pl.pallas_call(
        functools.partial(_bwd_kernel, nb=nb, scale=scale),
        grid=(slots, nb),
        in_specs=[row, full, full, brow, row, row],
        out_specs=[row, full, full],
        out_shape=(shape, shape, shape),
        scratch_shapes=[pltpu.VMEM((length, hd), jnp.float32), pltpu.VMEM((length, hd), jnp.float32)],
        compiler_params=pltpu.CompilerParams(dimension_semantics=("arbitrary", "arbitrary")),
        interpret=interpret,
    )(q, k, v, bias, o, do)


def slot_table(head_owner, most_slots, seq_count):
    head_count = head_owner.shape[0]
    same_owner = head_owner[:, None] == head_owner[None, :]
    earlier = jnp.arange(head_count)[None, :] < jnp.arange(head_count)[:, None]
    owner_rank = jnp.sum(jnp.logical_and(same_owner, earlier), axis=1)
    slot_index = head_owner * most_slots + owner_rank
    return slot_index[:, None] == jnp.arange(seq_count * most_slots, dtype=jnp.int32)[None, :]


def heads_to_tokens(received, select, token_count, head_count, head_dim):
    merged = jnp.einsum("jtd,hj->thd", received[:, 0], select, preferred_element_type=jnp.float32)
    return merged.astype(jnp.bfloat16).reshape(1, token_count, head_count * head_dim)


def on_device(query_tok, key_tok, value_tok, grad_out, out_weight, block_mask, head_owner):
    seq_count = lax.axis_size("seq")
    most_slots = out_weight.shape[0]
    head_dim = out_weight.shape[1]
    token_count = query_tok.shape[1]
    head_count = block_mask.shape[0]
    length = seq_count * token_count
    score_scale = head_dim ** (-0.5)
    grad_scale = (lax.axis_size("dp") * length) ** (-0.5)
    table = slot_table(head_owner, most_slots, seq_count)
    select = table.astype(jnp.bfloat16)
    my_first = lax.axis_index("seq") * most_slots
    local_select = lax.dynamic_slice_in_dim(table.astype(jnp.float32), my_first, most_slots, 1)
    slot_blocks = jnp.einsum("hs,hab->sab", local_select, block_mask.astype(jnp.float32))
    slot_used = jnp.sum(local_select, axis=0)
    diagonal = jnp.eye(block_mask.shape[1], dtype=jnp.float32)
    slot_blocks = slot_blocks + (1.0 - slot_used)[:, None, None] * diagonal[None]
    slot_mask = (slot_blocks > 0.5).astype(jnp.int32)
    bias = mask_bias(slot_mask, length)

    def to_slots(tensor):
        split_heads = tensor[0].reshape(token_count, head_count, head_dim)
        spread = jnp.einsum("thd,hj->jtd", split_heads, select, preferred_element_type=jnp.float32)
        return spread.astype(jnp.bfloat16).reshape(seq_count, most_slots, token_count, head_dim)

    stacked = jnp.stack([to_slots(query_tok), to_slots(key_tok), to_slots(value_tok)], axis=1)
    arrived = lax.all_to_all(stacked, "seq", split_axis=0, concat_axis=3, tiled=True)[0]
    slot_query = arrived[0]
    slot_key = arrived[1]
    slot_value = arrived[2]
    dp_count = lax.axis_size("dp")
    weight_copies = jnp.broadcast_to(out_weight[None], (dp_count,) + out_weight.shape)
    weight_parts = lax.all_to_all(weight_copies, "dp", split_axis=0, concat_axis=0, tiled=True)
    slot_out = attn_forward(bias, slot_query, slot_key, slot_value, score_scale)

    def back_layout(stacked):
        return stacked.reshape(most_slots, seq_count, token_count, head_dim)

    weight_full = jnp.transpose(weight_parts, (1, 2, 0, 3)).reshape(
        most_slots, head_dim, dp_count * out_weight.shape[2]
    )
    dy_rows = lax.all_gather(grad_out, "seq", axis=1, tiled=True)[0]
    part = jnp.einsum(
        "td,shd->sth", dy_rows, weight_full, preferred_element_type=jnp.float32
    ).astype(jnp.bfloat16)
    grad_attn = part
    weight_total = jnp.einsum("sth,td->shd", slot_out, dy_rows, preferred_element_type=jnp.float32)
    grad_attn, weight_total = (grad_attn, weight_total)
    weight_grad = lax.psum_scatter(
        (weight_total * grad_scale).astype(jnp.bfloat16), "dp", scatter_dimension=2, tiled=True
    ).astype(jnp.float32)
    grads_parts = []
    for slot_number in range(most_slots):
        one = slice(slot_number, slot_number + 1)
        slot_grads = attn_backward(
            bias[one],
            slot_query[one],
            slot_key[one],
            slot_value[one],
            slot_out[one],
            grad_attn[one],
            score_scale,
        )
        one_stack = jnp.stack(
            [g.reshape(1, seq_count, token_count, head_dim) for g in (slot_out[one],) + tuple(slot_grads)]
        )
        grads_parts.append(lax.all_to_all(one_stack, "seq", split_axis=2, concat_axis=1, tiled=True))
    grads_back = jnp.stack(grads_parts, axis=2).reshape(4, seq_count * most_slots, 1, token_count, head_dim)
    all_back = (grads_back[0], grads_back[1], grads_back[2], grads_back[3])
    attn_out = heads_to_tokens(all_back[0], select, token_count, head_count, head_dim)
    query_grad = heads_to_tokens(all_back[1], select, token_count, head_count, head_dim)
    key_grad = heads_to_tokens(all_back[2], select, token_count, head_count, head_dim)
    value_grad = heads_to_tokens(all_back[3], select, token_count, head_count, head_dim)
    return (attn_out, query_grad, key_grad, value_grad, weight_grad)


def solution(mesh):
    placed = (
        P("dp", "seq", None),
        P("dp", "seq", None),
        P("dp", "seq", None),
        P("dp", "seq", None),
        P("seq", None, "dp"),
        P(),
        P(),
    )
    return jax.shard_map(
        on_device,
        mesh=mesh,
        in_specs=placed,
        out_specs=(
            P("dp", "seq", None),
            P("dp", "seq", None),
            P("dp", "seq", None),
            P("dp", "seq", None),
            P("seq", None, "dp"),
        ),
        check_vma=False,
    )
```

```python
import jax
import jax.numpy as jnp
from jax import lax
from jax.sharding import PartitionSpec as P
import functools
from jax.experimental import pallas as pl
from jax.experimental.pallas import tpu as pltpu


TILE = 128
NT = (((1,), (1,)), ((), ()))
TN = (((0,), (0,)), ((), ()))


def _probs(q, k, bias, scale):
    sc = lax.dot_general(q, k, NT, preferred_element_type=jnp.float32) * scale + bias
    e = jnp.exp(sc - jnp.max(sc, axis=1, keepdims=True))
    return e * (1.0 / jnp.sum(e, axis=1, keepdims=True))


def _fwd_kernel(q_ref, k_ref, v_ref, b_ref, o_ref, *, scale):
    prob = _probs(q_ref[0], k_ref[0], b_ref[0, 0], scale)
    out = jnp.dot(prob.astype(jnp.bfloat16), v_ref[0], preferred_element_type=jnp.float32)
    o_ref[0] = out.astype(o_ref.dtype)


def _bwd_kernel(q_ref, k_ref, v_ref, b_ref, o_ref, do_ref, dq_ref, dk_ref, dv_ref,
                dk_scr, dv_scr, *, nb, scale):
    qi = pl.program_id(1)

    @pl.when(qi == 0)
    def _():
        dk_scr[...] = jnp.zeros(dk_scr.shape, jnp.float32)
        dv_scr[...] = jnp.zeros(dv_scr.shape, jnp.float32)

    q = q_ref[0]
    k = k_ref[0]
    v = v_ref[0]
    do = do_ref[0]
    prob = _probs(q, k, b_ref[0, 0], scale)
    low = prob.astype(jnp.bfloat16)
    delta = jnp.sum(do.astype(jnp.float32) * o_ref[0].astype(jnp.float32), axis=1, keepdims=True)
    dv_scr[...] += lax.dot_general(low, do, TN, preferred_element_type=jnp.float32)
    dp = lax.dot_general(do, v, NT, preferred_element_type=jnp.float32)
    ds = (prob * (dp - delta) * scale).astype(jnp.bfloat16)
    dq_ref[0] = jnp.dot(ds, k, preferred_element_type=jnp.float32).astype(dq_ref.dtype)
    dk_scr[...] += lax.dot_general(ds, q, TN, preferred_element_type=jnp.float32)

    @pl.when(qi == nb - 1)
    def _():
        dk_ref[0] = dk_scr[...].astype(dk_ref.dtype)
        dv_ref[0] = dv_scr[...].astype(dv_ref.dtype)


def mask_bias(slot_mask, length):
    spread = jnp.repeat(slot_mask, length // slot_mask.shape[2], axis=2)
    return jnp.where(spread > 0, 0.0, -jnp.inf).astype(jnp.float32)[:, :, None, :]


def attn_forward(bias, q, k, v, scale, interpret=False):
    slots, length, hd = q.shape
    nb = length // TILE
    row = pl.BlockSpec((1, TILE, hd), lambda s, i: (s, i, 0))
    full = pl.BlockSpec((1, length, hd), lambda s, i: (s, 0, 0))
    brow = pl.BlockSpec((1, 1, 1, length), lambda s, i: (s, i, 0, 0))
    return pl.pallas_call(
        functools.partial(_fwd_kernel, scale=scale),
        grid=(slots, nb),
        in_specs=[row, full, full, brow],
        out_specs=row,
        out_shape=jax.ShapeDtypeStruct(q.shape, jnp.bfloat16),
        compiler_params=pltpu.CompilerParams(dimension_semantics=("arbitrary", "arbitrary")),
        interpret=interpret,
    )(q, k, v, bias)


def attn_backward(bias, q, k, v, o, do, scale, interpret=False):
    slots, length, hd = q.shape
    nb = length // TILE
    row = pl.BlockSpec((1, TILE, hd), lambda s, i: (s, i, 0))
    full = pl.BlockSpec((1, length, hd), lambda s, i: (s, 0, 0))
    brow = pl.BlockSpec((1, 1, 1, length), lambda s, i: (s, i, 0, 0))
    shape = jax.ShapeDtypeStruct(q.shape, jnp.bfloat16)
    return pl.pallas_call(
        functools.partial(_bwd_kernel, nb=nb, scale=scale),
        grid=(slots, nb),
        in_specs=[row, full, full, brow, row, row],
        out_specs=[row, full, full],
        out_shape=(shape, shape, shape),
        scratch_shapes=[pltpu.VMEM((length, hd), jnp.float32), pltpu.VMEM((length, hd), jnp.float32)],
        compiler_params=pltpu.CompilerParams(dimension_semantics=("arbitrary", "arbitrary")),
        interpret=interpret,
    )(q, k, v, bias, o, do)


def slot_table(head_owner, most_slots, seq_count):
    head_count = head_owner.shape[0]
    same_owner = head_owner[:, None] == head_owner[None, :]
    earlier = jnp.arange(head_count)[None, :] < jnp.arange(head_count)[:, None]
    owner_rank = jnp.sum(jnp.logical_and(same_owner, earlier), axis=1)
    slot_index = head_owner * most_slots + owner_rank
    return slot_index[:, None] == jnp.arange(seq_count * most_slots, dtype=jnp.int32)[None, :]


def heads_to_tokens(received, select, token_count, head_count, head_dim):
    merged = jnp.einsum("jtd,hj->thd", received[:, 0], select, preferred_element_type=jnp.float32)
    return merged.astype(jnp.bfloat16).reshape(1, token_count, head_count * head_dim)


def on_device(query_tok, key_tok, value_tok, grad_out, out_weight, block_mask, head_owner):
    seq_count = lax.axis_size("seq")
    most_slots = out_weight.shape[0]
    head_dim = out_weight.shape[1]
    token_count = query_tok.shape[1]
    head_count = block_mask.shape[0]
    length = seq_count * token_count
    score_scale = head_dim ** (-0.5)
    grad_scale = (lax.axis_size("dp") * length) ** (-0.5)
    table = slot_table(head_owner, most_slots, seq_count)
    select = table.astype(jnp.bfloat16)
    my_first = lax.axis_index("seq") * most_slots
    local_select = lax.dynamic_slice_in_dim(table.astype(jnp.float32), my_first, most_slots, 1)
    slot_blocks = jnp.einsum("hs,hab->sab", local_select, block_mask.astype(jnp.float32))
    slot_used = jnp.sum(local_select, axis=0)
    diagonal = jnp.eye(block_mask.shape[1], dtype=jnp.float32)
    slot_blocks = slot_blocks + (1.0 - slot_used)[:, None, None] * diagonal[None]
    slot_mask = (slot_blocks > 0.5).astype(jnp.int32)
    bias = mask_bias(slot_mask, length)

    def to_slots(tensor):
        split_heads = tensor[0].reshape(token_count, head_count, head_dim)
        spread = jnp.einsum("thd,hj->jtd", split_heads, select, preferred_element_type=jnp.float32)
        return spread.astype(jnp.bfloat16).reshape(seq_count, most_slots, token_count, head_dim)

    stacked = jnp.stack([to_slots(query_tok), to_slots(key_tok), to_slots(value_tok)], axis=1)
    arrived = lax.all_to_all(stacked, "seq", split_axis=0, concat_axis=3, tiled=True)[0]
    slot_query = arrived[0]
    slot_key = arrived[1]
    slot_value = arrived[2]
    dp_count = lax.axis_size("dp")
    weight_copies = jnp.broadcast_to(out_weight[None], (dp_count,) + out_weight.shape)
    weight_parts = lax.all_to_all(weight_copies, "dp", split_axis=0, concat_axis=0, tiled=True)
    slot_out = attn_forward(bias, slot_query, slot_key, slot_value, score_scale)

    def back_layout(stacked):
        return stacked.reshape(most_slots, seq_count, token_count, head_dim)

    weight_full = jnp.transpose(weight_parts, (1, 2, 0, 3)).reshape(
        most_slots, head_dim, dp_count * out_weight.shape[2]
    )
    half = grad_out.shape[2] // 2
    dy_first = lax.all_gather(grad_out[:, :, :half], "seq", axis=1, tiled=True)[0]
    dy_second = lax.all_gather(grad_out[:, :, half:], "seq", axis=1, tiled=True)[0]
    part = (
        jnp.einsum("td,shd->sth", dy_first, weight_full[:, :, :half], preferred_element_type=jnp.float32)
        + jnp.einsum("td,shd->sth", dy_second, weight_full[:, :, half:], preferred_element_type=jnp.float32)
    ).astype(jnp.bfloat16)
    grad_attn = part
    weight_total = jnp.concatenate(
        [
            jnp.einsum("sth,td->shd", slot_out, dy_first, preferred_element_type=jnp.float32),
            jnp.einsum("sth,td->shd", slot_out, dy_second, preferred_element_type=jnp.float32),
        ],
        axis=2,
    )
    grad_attn, weight_total = (grad_attn, weight_total)
    weight_grad = lax.psum_scatter(
        (weight_total * grad_scale).astype(jnp.bfloat16), "dp", scatter_dimension=2, tiled=True
    ).astype(jnp.float32)
    grads_parts = []
    for slot_number in range(most_slots):
        one = slice(slot_number, slot_number + 1)
        slot_grads = attn_backward(
            bias[one],
            slot_query[one],
            slot_key[one],
            slot_value[one],
            slot_out[one],
            grad_attn[one],
            score_scale,
        )
        one_stack = jnp.stack(
            [g.reshape(1, seq_count, token_count, head_dim) for g in (slot_out[one],) + tuple(slot_grads)]
        )
        grads_parts.append(lax.all_to_all(one_stack, "seq", split_axis=2, concat_axis=1, tiled=True))
    grads_back = jnp.stack(grads_parts, axis=2).reshape(4, seq_count * most_slots, 1, token_count, head_dim)
    all_back = (grads_back[0], grads_back[1], grads_back[2], grads_back[3])
    attn_out = heads_to_tokens(all_back[0], select, token_count, head_count, head_dim)
    query_grad = heads_to_tokens(all_back[1], select, token_count, head_count, head_dim)
    key_grad = heads_to_tokens(all_back[2], select, token_count, head_count, head_dim)
    value_grad = heads_to_tokens(all_back[3], select, token_count, head_count, head_dim)
    return (attn_out, query_grad, key_grad, value_grad, weight_grad)


def solution(mesh):
    placed = (
        P("dp", "seq", None),
        P("dp", "seq", None),
        P("dp", "seq", None),
        P("dp", "seq", None),
        P("seq", None, "dp"),
        P(),
        P(),
    )
    return jax.shard_map(
        on_device,
        mesh=mesh,
        in_specs=placed,
        out_specs=(
            P("dp", "seq", None),
            P("dp", "seq", None),
            P("dp", "seq", None),
            P("dp", "seq", None),
            P("seq", None, "dp"),
        ),
        check_vma=False,
    )
```

```python
import jax
import jax.numpy as jnp
from jax import lax
from jax.sharding import PartitionSpec as P
import functools
from jax.experimental import pallas as pl
from jax.experimental.pallas import tpu as pltpu


TILE = 128
NT = (((1,), (1,)), ((), ()))
TN = (((0,), (0,)), ((), ()))


def _probs(q, k, bias, scale):
    sc = lax.dot_general(q, k, NT, preferred_element_type=jnp.float32) * scale + bias
    e = jnp.exp(sc - jnp.max(sc, axis=1, keepdims=True))
    return e / jnp.sum(e, axis=1, keepdims=True)


def _fwd_kernel(q_ref, k_ref, v_ref, b_ref, o_ref, p_ref, *, scale):
    prob = _probs(q_ref[0], k_ref[0], b_ref[0, 0], scale)
    p_ref[0] = prob
    out = jnp.dot(prob.astype(jnp.bfloat16), v_ref[0], preferred_element_type=jnp.float32)
    o_ref[0] = out.astype(o_ref.dtype)


def _bwd_kernel(q_ref, k_ref, v_ref, p_ref, o_ref, do_ref, dq_ref, dk_ref, dv_ref,
                dk_scr, dv_scr, *, nb, scale):
    qi = pl.program_id(0)

    @pl.when(qi == 0)
    def _():
        dk_scr[...] = jnp.zeros(dk_scr.shape, jnp.float32)
        dv_scr[...] = jnp.zeros(dv_scr.shape, jnp.float32)

    q = q_ref[0]
    k = k_ref[0]
    v = v_ref[0]
    do = do_ref[0]
    prob = p_ref[0]
    low = prob.astype(jnp.bfloat16)
    delta = jnp.sum(do.astype(jnp.float32) * o_ref[0].astype(jnp.float32), axis=1, keepdims=True)
    dv_scr[...] += lax.dot_general(low, do, TN, preferred_element_type=jnp.float32)
    dp = lax.dot_general(do, v, NT, preferred_element_type=jnp.float32)
    ds = (prob * (dp - delta) * scale).astype(jnp.bfloat16)
    dq_ref[0] = jnp.dot(ds, k, preferred_element_type=jnp.float32).astype(dq_ref.dtype)
    dk_scr[...] += lax.dot_general(ds, q, TN, preferred_element_type=jnp.float32)

    @pl.when(qi == nb - 1)
    def _():
        dk_ref[0] = dk_scr[...].astype(dk_ref.dtype)
        dv_ref[0] = dv_scr[...].astype(dv_ref.dtype)


def mask_bias(slot_mask, length):
    spread = jnp.repeat(slot_mask, length // slot_mask.shape[2], axis=2)
    return jnp.where(spread > 0, 0.0, -jnp.inf).astype(jnp.float32)[:, :, None, :]


def attn_forward(bias, q, k, v, scale):
    slots, length, hd = q.shape
    nb = length // TILE
    row = pl.BlockSpec((1, TILE, hd), lambda s, i: (s, i, 0))
    full = pl.BlockSpec((1, length, hd), lambda s, i: (s, 0, 0))
    brow = pl.BlockSpec((1, 1, 1, length), lambda s, i: (s, i, 0, 0))
    prow = pl.BlockSpec((1, TILE, length), lambda s, i: (s, i, 0))
    return pl.pallas_call(
        functools.partial(_fwd_kernel, scale=scale),
        grid=(slots, nb),
        in_specs=[row, full, full, brow],
        out_specs=[row, prow],
        out_shape=(
            jax.ShapeDtypeStruct(q.shape, jnp.bfloat16),
            jax.ShapeDtypeStruct((slots, length, length), jnp.float32),
        ),
        compiler_params=pltpu.CompilerParams(dimension_semantics=("arbitrary", "arbitrary")),
    )(q, k, v, bias)


def attn_backward(prob, q, k, v, o, do, scale, slot):
    slots, length, hd = q.shape
    nb = length // TILE
    row = pl.BlockSpec((1, TILE, hd), lambda i: (slot, i, 0))
    full = pl.BlockSpec((1, length, hd), lambda i: (slot, 0, 0))
    prow = pl.BlockSpec((1, TILE, length), lambda i: (slot, i, 0))
    out_row = pl.BlockSpec((1, TILE, hd), lambda i: (0, i, 0))
    out_full = pl.BlockSpec((1, length, hd), lambda i: (0, 0, 0))
    shape = jax.ShapeDtypeStruct((1, length, hd), jnp.bfloat16)
    return pl.pallas_call(
        functools.partial(_bwd_kernel, nb=nb, scale=scale),
        grid=(nb,),
        in_specs=[row, full, full, prow, row, row],
        out_specs=[out_row, out_full, out_full],
        out_shape=(shape, shape, shape),
        scratch_shapes=[pltpu.VMEM((length, hd), jnp.float32), pltpu.VMEM((length, hd), jnp.float32)],
        compiler_params=pltpu.CompilerParams(dimension_semantics=("arbitrary",)),
    )(q, k, v, prob, o, do)


def slot_table(head_owner, most_slots, seq_count):
    head_count = head_owner.shape[0]
    same_owner = head_owner[:, None] == head_owner[None, :]
    earlier = jnp.arange(head_count)[None, :] < jnp.arange(head_count)[:, None]
    owner_rank = jnp.sum(jnp.logical_and(same_owner, earlier), axis=1)
    slot_index = head_owner * most_slots + owner_rank
    return slot_index[:, None] == jnp.arange(seq_count * most_slots, dtype=jnp.int32)[None, :]


def heads_to_tokens(received, select, token_count, head_count, head_dim):
    merged = jnp.einsum("jtd,hj->thd", received[:, 0], select, preferred_element_type=jnp.float32)
    return merged.astype(jnp.bfloat16).reshape(1, token_count, head_count * head_dim)


def on_device(query_tok, key_tok, value_tok, grad_out, out_weight, block_mask, head_owner):
    seq_count = lax.axis_size("seq")
    most_slots = out_weight.shape[0]
    head_dim = out_weight.shape[1]
    token_count = query_tok.shape[1]
    head_count = block_mask.shape[0]
    length = seq_count * token_count
    score_scale = head_dim ** (-0.5)
    grad_scale = (lax.axis_size("dp") * length) ** (-0.5)
    table = slot_table(head_owner, most_slots, seq_count)
    select = table.astype(jnp.bfloat16)
    my_first = lax.axis_index("seq") * most_slots
    local_select = lax.dynamic_slice_in_dim(table.astype(jnp.float32), my_first, most_slots, 1)
    slot_blocks = jnp.einsum("hs,hab->sab", local_select, block_mask.astype(jnp.float32))
    slot_used = jnp.sum(local_select, axis=0)
    diagonal = jnp.eye(block_mask.shape[1], dtype=jnp.float32)
    slot_blocks = slot_blocks + (1.0 - slot_used)[:, None, None] * diagonal[None]
    slot_mask = (slot_blocks > 0.5).astype(jnp.int32)
    bias = mask_bias(slot_mask, length)

    def to_slots(tensor):
        split_heads = tensor[0].reshape(token_count, head_count, head_dim)
        spread = jnp.einsum("thd,hj->jtd", split_heads, select, preferred_element_type=jnp.float32)
        return spread.astype(jnp.bfloat16).reshape(seq_count, most_slots, token_count, head_dim)

    stacked = jnp.stack([to_slots(query_tok), to_slots(key_tok), to_slots(value_tok)], axis=1)
    arrived = lax.all_to_all(stacked, "seq", split_axis=0, concat_axis=3, tiled=True)[0]
    slot_query = arrived[0]
    slot_key = arrived[1]
    slot_value = arrived[2]
    dp_count = lax.axis_size("dp")
    weight_copies = jnp.broadcast_to(out_weight[None], (dp_count,) + out_weight.shape)
    weight_parts = lax.all_to_all(weight_copies, "dp", split_axis=0, concat_axis=0, tiled=True)
    slot_out, slot_prob = attn_forward(bias, slot_query, slot_key, slot_value, score_scale)

    def back_layout(stacked):
        return stacked.reshape(most_slots, seq_count, token_count, head_dim)

    weight_full = jnp.transpose(weight_parts, (1, 2, 0, 3)).reshape(
        most_slots, head_dim, dp_count * out_weight.shape[2]
    )
    dy_rows = lax.all_gather(grad_out, "seq", axis=1, tiled=True)[0]
    part = jnp.einsum(
        "td,shd->sth", dy_rows, weight_full, preferred_element_type=jnp.float32
    ).astype(jnp.bfloat16)
    grad_attn = part
    weight_total = jnp.einsum("sth,td->shd", slot_out, dy_rows, preferred_element_type=jnp.float32)
    grad_attn, weight_total = (grad_attn, weight_total)
    weight_grad = lax.psum_scatter(
        (weight_total * grad_scale).astype(jnp.bfloat16), "dp", scatter_dimension=2, tiled=True
    ).astype(jnp.float32)
    def to_owners(tensors):
        one_stack = jnp.stack([t.reshape(seq_count, token_count, head_dim) for t in tensors])
        return lax.all_to_all(one_stack, "seq", split_axis=1, concat_axis=1, tiled=True)

    sent = []
    for slot_number in range(most_slots):
        slot_grads = attn_backward(
            slot_prob, slot_query, slot_key, slot_value, slot_out, grad_attn, score_scale, slot_number
        )
        if slot_number == 0:
            sent.append(to_owners(tuple(slot_out) + tuple(slot_grads)))
        else:
            sent.append(to_owners(slot_grads))
    base = most_slots

    def merged(pieces):
        return jnp.stack(pieces, axis=1).reshape(seq_count * most_slots, 1, token_count, head_dim)

    all_back = [merged([sent[0][number] for number in range(most_slots)])]
    for which in range(3):
        all_back.append(
            merged([sent[0][base + which]] + [sent[number][which] for number in range(1, most_slots)])
        )
    attn_out = heads_to_tokens(all_back[0], select, token_count, head_count, head_dim)
    query_grad = heads_to_tokens(all_back[1], select, token_count, head_count, head_dim)
    key_grad = heads_to_tokens(all_back[2], select, token_count, head_count, head_dim)
    value_grad = heads_to_tokens(all_back[3], select, token_count, head_count, head_dim)
    return (attn_out, query_grad, key_grad, value_grad, weight_grad)


def solution(mesh):
    placed = (
        P("dp", "seq", None),
        P("dp", "seq", None),
        P("dp", "seq", None),
        P("dp", "seq", None),
        P("seq", None, "dp"),
        P(),
        P(),
    )
    return jax.shard_map(
        on_device,
        mesh=mesh,
        in_specs=placed,
        out_specs=(
            P("dp", "seq", None),
            P("dp", "seq", None),
            P("dp", "seq", None),
            P("dp", "seq", None),
            P("seq", None, "dp"),
        ),
        check_vma=False,
    )
```

```python
import jax
import jax.numpy as jnp
from jax import lax
from jax.sharding import PartitionSpec as P
import functools
from jax.experimental import pallas as pl
from jax.experimental.pallas import tpu as pltpu


TILE = 128
NT = (((1,), (1,)), ((), ()))
TN = (((0,), (0,)), ((), ()))


def _probs(q, k, bias, scale):
    sc = lax.dot_general(q, k, NT, preferred_element_type=jnp.float32) * scale + bias
    e = jnp.exp(sc - jnp.max(sc, axis=1, keepdims=True))
    return e / jnp.sum(e, axis=1, keepdims=True)


def _fwd_kernel(q_ref, k_ref, v_ref, b_ref, o_ref, p_ref, *, scale):
    prob = _probs(q_ref[0], k_ref[0], b_ref[0, 0], scale)
    p_ref[0] = prob
    out = jnp.dot(prob.astype(jnp.bfloat16), v_ref[0], preferred_element_type=jnp.float32)
    o_ref[0] = out.astype(o_ref.dtype)


def _bwd_kernel(q_ref, k_ref, v_ref, p_ref, o_ref, do_ref, dq_ref, dk_ref, dv_ref,
                dk_scr, dv_scr, *, nb, scale):
    qi = pl.program_id(0)

    @pl.when(qi == 0)
    def _():
        dk_scr[...] = jnp.zeros(dk_scr.shape, jnp.float32)
        dv_scr[...] = jnp.zeros(dv_scr.shape, jnp.float32)

    q = q_ref[0]
    k = k_ref[0]
    v = v_ref[0]
    do = do_ref[0]
    prob = p_ref[0]
    low = prob.astype(jnp.bfloat16)
    delta = jnp.sum(do.astype(jnp.float32) * o_ref[0].astype(jnp.float32), axis=1, keepdims=True)
    dv_scr[...] += lax.dot_general(low, do, TN, preferred_element_type=jnp.float32)
    dp = lax.dot_general(do, v, NT, preferred_element_type=jnp.float32)
    ds = (prob * (dp - delta) * scale).astype(jnp.bfloat16)
    dq_ref[0] = jnp.dot(ds, k, preferred_element_type=jnp.float32).astype(dq_ref.dtype)
    dk_scr[...] += lax.dot_general(ds, q, TN, preferred_element_type=jnp.float32)

    @pl.when(qi == nb - 1)
    def _():
        dk_ref[0] = dk_scr[...].astype(dk_ref.dtype)
        dv_ref[0] = dv_scr[...].astype(dv_ref.dtype)


def mask_bias(slot_mask, length):
    spread = jnp.repeat(slot_mask, length // slot_mask.shape[2], axis=2)
    return jnp.where(spread > 0, 0.0, -jnp.inf).astype(jnp.float32)[:, :, None, :]


def attn_forward(bias, q, k, v, scale):
    slots, length, hd = q.shape
    nb = length // TILE
    row = pl.BlockSpec((1, TILE, hd), lambda s, i: (s, i, 0))
    full = pl.BlockSpec((1, length, hd), lambda s, i: (s, 0, 0))
    brow = pl.BlockSpec((1, 1, 1, length), lambda s, i: (s, i, 0, 0))
    prow = pl.BlockSpec((1, TILE, length), lambda s, i: (s, i, 0))
    return pl.pallas_call(
        functools.partial(_fwd_kernel, scale=scale),
        grid=(slots, nb),
        in_specs=[row, full, full, brow],
        out_specs=[row, prow],
        out_shape=(
            jax.ShapeDtypeStruct(q.shape, jnp.bfloat16),
            jax.ShapeDtypeStruct((slots, length, length), jnp.float32),
        ),
        compiler_params=pltpu.CompilerParams(dimension_semantics=("arbitrary", "arbitrary")),
    )(q, k, v, bias)


def attn_backward(prob, q, k, v, o, do, scale, slot):
    slots, length, hd = q.shape
    nb = length // TILE
    row = pl.BlockSpec((1, TILE, hd), lambda i: (slot, i, 0))
    full = pl.BlockSpec((1, length, hd), lambda i: (slot, 0, 0))
    prow = pl.BlockSpec((1, TILE, length), lambda i: (slot, i, 0))
    out_row = pl.BlockSpec((1, TILE, hd), lambda i: (0, i, 0))
    out_full = pl.BlockSpec((1, length, hd), lambda i: (0, 0, 0))
    shape = jax.ShapeDtypeStruct((1, length, hd), jnp.bfloat16)
    return pl.pallas_call(
        functools.partial(_bwd_kernel, nb=nb, scale=scale),
        grid=(nb,),
        in_specs=[row, full, full, prow, row, row],
        out_specs=[out_row, out_full, out_full],
        out_shape=(shape, shape, shape),
        scratch_shapes=[pltpu.VMEM((length, hd), jnp.float32), pltpu.VMEM((length, hd), jnp.float32)],
        compiler_params=pltpu.CompilerParams(dimension_semantics=("arbitrary",)),
    )(q, k, v, prob, o, do)


def slot_table(head_owner, most_slots, seq_count):
    head_count = head_owner.shape[0]
    same_owner = head_owner[:, None] == head_owner[None, :]
    earlier = jnp.arange(head_count)[None, :] < jnp.arange(head_count)[:, None]
    owner_rank = jnp.sum(jnp.logical_and(same_owner, earlier), axis=1)
    slot_index = head_owner * most_slots + owner_rank
    return slot_index[:, None] == jnp.arange(seq_count * most_slots, dtype=jnp.int32)[None, :]


def heads_to_tokens(received, select, token_count, head_count, head_dim):
    merged = jnp.einsum("jtd,hj->thd", received[:, 0], select, preferred_element_type=jnp.float32)
    return merged.astype(jnp.bfloat16).reshape(1, token_count, head_count * head_dim)


def on_device(query_tok, key_tok, value_tok, grad_out, out_weight, block_mask, head_owner):
    seq_count = lax.axis_size("seq")
    most_slots = out_weight.shape[0]
    head_dim = out_weight.shape[1]
    token_count = query_tok.shape[1]
    head_count = block_mask.shape[0]
    length = seq_count * token_count
    score_scale = head_dim ** (-0.5)
    grad_scale = (lax.axis_size("dp") * length) ** (-0.5)
    table = slot_table(head_owner, most_slots, seq_count)
    select = table.astype(jnp.bfloat16)
    my_first = lax.axis_index("seq") * most_slots
    local_select = lax.dynamic_slice_in_dim(table.astype(jnp.float32), my_first, most_slots, 1)
    slot_blocks = jnp.einsum("hs,hab->sab", local_select, block_mask.astype(jnp.float32))
    slot_used = jnp.sum(local_select, axis=0)
    diagonal = jnp.eye(block_mask.shape[1], dtype=jnp.float32)
    slot_blocks = slot_blocks + (1.0 - slot_used)[:, None, None] * diagonal[None]
    slot_mask = (slot_blocks > 0.5).astype(jnp.int32)
    bias = mask_bias(slot_mask, length)

    def to_slots(tensor):
        split_heads = tensor[0].reshape(token_count, head_count, head_dim)
        spread = jnp.einsum("thd,hj->jtd", split_heads, select, preferred_element_type=jnp.float32)
        return spread.astype(jnp.bfloat16).reshape(seq_count, most_slots, token_count, head_dim)

    stacked = jnp.stack([to_slots(query_tok), to_slots(key_tok), to_slots(value_tok)], axis=1)
    arrived = lax.all_to_all(stacked, "seq", split_axis=0, concat_axis=3, tiled=True)[0]
    slot_query = arrived[0]
    slot_key = arrived[1]
    slot_value = arrived[2]
    dp_count = lax.axis_size("dp")
    weight_copies = jnp.broadcast_to(out_weight[None], (dp_count,) + out_weight.shape)
    weight_parts = lax.all_to_all(weight_copies, "dp", split_axis=0, concat_axis=0, tiled=True)
    slot_out, slot_prob = attn_forward(bias, slot_query, slot_key, slot_value, score_scale)

    def back_layout(stacked):
        return stacked.reshape(most_slots, seq_count, token_count, head_dim)

    weight_full = jnp.transpose(weight_parts, (1, 2, 0, 3)).reshape(
        most_slots, head_dim, dp_count * out_weight.shape[2]
    )
    dy_rows = lax.all_gather(grad_out, "seq", axis=1, tiled=True)[0]
    part = jnp.einsum(
        "td,shd->sth", dy_rows, weight_full, preferred_element_type=jnp.float32
    ).astype(jnp.bfloat16)
    grad_attn = part
    weight_total = jnp.einsum("sth,td->shd", slot_out, dy_rows, preferred_element_type=jnp.float32)
    grad_attn, weight_total = lax.optimization_barrier((grad_attn, weight_total))
    weight_grad = lax.psum_scatter(
        (weight_total * grad_scale).astype(jnp.bfloat16), "dp", scatter_dimension=2, tiled=True
    ).astype(jnp.float32)
    def to_owners(tensors):
        one_stack = jnp.stack([t.reshape(seq_count, token_count, head_dim) for t in tensors])
        return lax.all_to_all(one_stack, "seq", split_axis=1, concat_axis=1, tiled=True)

    sent = []
    for slot_number in range(most_slots):
        slot_grads = attn_backward(
            slot_prob, slot_query, slot_key, slot_value, slot_out, grad_attn, score_scale, slot_number
        )
        if slot_number == 0:
            sent.append(to_owners(tuple(slot_out) + tuple(slot_grads)))
        else:
            sent.append(to_owners(slot_grads))
    base = most_slots

    def merged(pieces):
        return jnp.stack(pieces, axis=1).reshape(seq_count * most_slots, 1, token_count, head_dim)

    all_back = [merged([sent[0][number] for number in range(most_slots)])]
    for which in range(3):
        all_back.append(
            merged([sent[0][base + which]] + [sent[number][which] for number in range(1, most_slots)])
        )
    attn_out = heads_to_tokens(all_back[0], select, token_count, head_count, head_dim)
    query_grad = heads_to_tokens(all_back[1], select, token_count, head_count, head_dim)
    key_grad = heads_to_tokens(all_back[2], select, token_count, head_count, head_dim)
    value_grad = heads_to_tokens(all_back[3], select, token_count, head_count, head_dim)
    return (attn_out, query_grad, key_grad, value_grad, weight_grad)


def solution(mesh):
    placed = (
        P("dp", "seq", None),
        P("dp", "seq", None),
        P("dp", "seq", None),
        P("dp", "seq", None),
        P("seq", None, "dp"),
        P(),
        P(),
    )
    return jax.shard_map(
        on_device,
        mesh=mesh,
        in_specs=placed,
        out_specs=(
            P("dp", "seq", None),
            P("dp", "seq", None),
            P("dp", "seq", None),
            P("dp", "seq", None),
            P("seq", None, "dp"),
        ),
        check_vma=False,
    )
```

```python
import jax
import jax.numpy as jnp
from jax import lax
from jax.sharding import PartitionSpec as P
import functools
from jax.experimental import pallas as pl
from jax.experimental.pallas import tpu as pltpu


TILE = 128
NT = (((1,), (1,)), ((), ()))
TN = (((0,), (0,)), ((), ()))


def _probs(q, k, bias, scale):
    sc = lax.dot_general(q, k, NT, preferred_element_type=jnp.float32) * scale + bias
    e = jnp.exp(sc - jnp.max(sc, axis=1, keepdims=True))
    return e / jnp.sum(e, axis=1, keepdims=True)


def _fwd_kernel(q_ref, k_ref, v_ref, b_ref, o_ref, p_ref, *, scale):
    prob = _probs(q_ref[0], k_ref[0], b_ref[0, 0], scale)
    p_ref[0] = prob
    out = jnp.dot(prob.astype(jnp.bfloat16), v_ref[0], preferred_element_type=jnp.float32)
    o_ref[0] = out.astype(o_ref.dtype)


def _bwd_kernel(q_ref, k_ref, v_ref, p_ref, o_ref, do_ref, dq_ref, dk_ref, dv_ref,
                dk_scr, dv_scr, *, nb, scale):
    qi = pl.program_id(0)

    @pl.when(qi == 0)
    def _():
        dk_scr[...] = jnp.zeros(dk_scr.shape, jnp.float32)
        dv_scr[...] = jnp.zeros(dv_scr.shape, jnp.float32)

    q = q_ref[0]
    k = k_ref[0]
    v = v_ref[0]
    do = do_ref[0]
    prob = p_ref[0]
    low = prob.astype(jnp.bfloat16)
    delta = jnp.sum(do.astype(jnp.float32) * o_ref[0].astype(jnp.float32), axis=1, keepdims=True)
    dv_scr[...] += lax.dot_general(low, do, TN, preferred_element_type=jnp.float32)
    dp = lax.dot_general(do, v, NT, preferred_element_type=jnp.float32)
    ds = (prob * (dp - delta) * scale).astype(jnp.bfloat16)
    dq_ref[0] = jnp.dot(ds, k, preferred_element_type=jnp.float32).astype(dq_ref.dtype)
    dk_scr[...] += lax.dot_general(ds, q, TN, preferred_element_type=jnp.float32)

    @pl.when(qi == nb - 1)
    def _():
        dk_ref[0] = dk_scr[...].astype(dk_ref.dtype)
        dv_ref[0] = dv_scr[...].astype(dv_ref.dtype)


def mask_bias(slot_mask, length):
    spread = jnp.repeat(slot_mask, length // slot_mask.shape[2], axis=2)
    return jnp.where(spread > 0, 0.0, -jnp.inf).astype(jnp.float32)[:, :, None, :]


def attn_forward(bias, q, k, v, scale):
    slots, length, hd = q.shape
    nb = length // TILE
    row = pl.BlockSpec((1, TILE, hd), lambda s, i: (s, i, 0))
    full = pl.BlockSpec((1, length, hd), lambda s, i: (s, 0, 0))
    brow = pl.BlockSpec((1, 1, 1, length), lambda s, i: (s, i, 0, 0))
    prow = pl.BlockSpec((1, TILE, length), lambda s, i: (s, i, 0))
    return pl.pallas_call(
        functools.partial(_fwd_kernel, scale=scale),
        grid=(slots, nb),
        in_specs=[row, full, full, brow],
        out_specs=[row, prow],
        out_shape=(
            jax.ShapeDtypeStruct(q.shape, jnp.bfloat16),
            jax.ShapeDtypeStruct((slots, length, length), jnp.float32),
        ),
        compiler_params=pltpu.CompilerParams(dimension_semantics=("arbitrary", "arbitrary")),
    )(q, k, v, bias)


def attn_backward(prob, q, k, v, o, do, scale, slot):
    slots, length, hd = q.shape
    nb = length // TILE
    row = pl.BlockSpec((1, TILE, hd), lambda i: (slot, i, 0))
    full = pl.BlockSpec((1, length, hd), lambda i: (slot, 0, 0))
    prow = pl.BlockSpec((1, TILE, length), lambda i: (slot, i, 0))
    out_row = pl.BlockSpec((1, TILE, hd), lambda i: (0, i, 0))
    out_full = pl.BlockSpec((1, length, hd), lambda i: (0, 0, 0))
    shape = jax.ShapeDtypeStruct((1, length, hd), jnp.bfloat16)
    return pl.pallas_call(
        functools.partial(_bwd_kernel, nb=nb, scale=scale),
        grid=(nb,),
        in_specs=[row, full, full, prow, row, row],
        out_specs=[out_row, out_full, out_full],
        out_shape=(shape, shape, shape),
        scratch_shapes=[pltpu.VMEM((length, hd), jnp.float32), pltpu.VMEM((length, hd), jnp.float32)],
        compiler_params=pltpu.CompilerParams(dimension_semantics=("arbitrary",)),
    )(q, k, v, prob, o, do)


def slot_table(head_owner, most_slots, seq_count):
    head_count = head_owner.shape[0]
    same_owner = head_owner[:, None] == head_owner[None, :]
    earlier = jnp.arange(head_count)[None, :] < jnp.arange(head_count)[:, None]
    owner_rank = jnp.sum(jnp.logical_and(same_owner, earlier), axis=1)
    slot_index = head_owner * most_slots + owner_rank
    return slot_index[:, None] == jnp.arange(seq_count * most_slots, dtype=jnp.int32)[None, :]


def heads_to_tokens(received, head_slots, token_count, head_count, head_dim):
    picked = jnp.take(received[:, 0], head_slots, axis=0)
    return jnp.transpose(picked, (1, 0, 2)).reshape(1, token_count, head_count * head_dim)


def on_device(query_tok, key_tok, value_tok, grad_out, out_weight, block_mask, head_owner):
    seq_count = lax.axis_size("seq")
    most_slots = out_weight.shape[0]
    head_dim = out_weight.shape[1]
    token_count = query_tok.shape[1]
    head_count = block_mask.shape[0]
    length = seq_count * token_count
    score_scale = head_dim ** (-0.5)
    grad_scale = (lax.axis_size("dp") * length) ** (-0.5)
    table = slot_table(head_owner, most_slots, seq_count)
    head_slots = jnp.argmax(table, axis=1).astype(jnp.int32)
    select = table.astype(jnp.bfloat16)
    my_first = lax.axis_index("seq") * most_slots
    local_select = lax.dynamic_slice_in_dim(table.astype(jnp.float32), my_first, most_slots, 1)
    slot_blocks = jnp.einsum("hs,hab->sab", local_select, block_mask.astype(jnp.float32))
    slot_used = jnp.sum(local_select, axis=0)
    diagonal = jnp.eye(block_mask.shape[1], dtype=jnp.float32)
    slot_blocks = slot_blocks + (1.0 - slot_used)[:, None, None] * diagonal[None]
    slot_mask = (slot_blocks > 0.5).astype(jnp.int32)
    bias = mask_bias(slot_mask, length)

    def to_slots(tensor):
        split_heads = tensor[0].reshape(token_count, head_count, head_dim)
        spread = jnp.einsum("thd,hj->jtd", split_heads, select, preferred_element_type=jnp.float32)
        return spread.astype(jnp.bfloat16).reshape(seq_count, most_slots, token_count, head_dim)

    stacked = jnp.stack([to_slots(query_tok), to_slots(key_tok), to_slots(value_tok)], axis=1)
    arrived = lax.all_to_all(stacked, "seq", split_axis=0, concat_axis=3, tiled=True)[0]
    slot_query = arrived[0]
    slot_key = arrived[1]
    slot_value = arrived[2]
    dp_count = lax.axis_size("dp")
    weight_copies = jnp.broadcast_to(out_weight[None], (dp_count,) + out_weight.shape)
    weight_parts = lax.all_to_all(weight_copies, "dp", split_axis=0, concat_axis=0, tiled=True)
    slot_out, slot_prob = attn_forward(bias, slot_query, slot_key, slot_value, score_scale)

    def back_layout(stacked):
        return stacked.reshape(most_slots, seq_count, token_count, head_dim)

    weight_full = jnp.transpose(weight_parts, (1, 2, 0, 3)).reshape(
        most_slots, head_dim, dp_count * out_weight.shape[2]
    )
    dy_rows = lax.all_gather(grad_out, "seq", axis=1, tiled=True)[0]
    part = jnp.einsum(
        "td,shd->sth", dy_rows, weight_full, preferred_element_type=jnp.float32
    ).astype(jnp.bfloat16)
    grad_attn = part
    weight_total = jnp.einsum("sth,td->shd", slot_out, dy_rows, preferred_element_type=jnp.float32)
    grad_attn, weight_total = lax.optimization_barrier((grad_attn, weight_total))
    weight_grad = lax.psum_scatter(
        (weight_total * grad_scale).astype(jnp.bfloat16), "dp", scatter_dimension=2, tiled=True
    ).astype(jnp.float32)
    def to_owners(tensors):
        one_stack = jnp.stack([t.reshape(seq_count, token_count, head_dim) for t in tensors])
        return lax.all_to_all(one_stack, "seq", split_axis=1, concat_axis=1, tiled=True)

    sent = []
    for slot_number in range(most_slots):
        slot_grads = attn_backward(
            slot_prob, slot_query, slot_key, slot_value, slot_out, grad_attn, score_scale, slot_number
        )
        if slot_number == 0:
            sent.append(to_owners(tuple(slot_out) + tuple(slot_grads)))
        else:
            sent.append(to_owners(slot_grads))
    base = most_slots

    def merged(pieces):
        return jnp.stack(pieces, axis=1).reshape(seq_count * most_slots, 1, token_count, head_dim)

    all_back = [merged([sent[0][number] for number in range(most_slots)])]
    for which in range(3):
        all_back.append(
            merged([sent[0][base + which]] + [sent[number][which] for number in range(1, most_slots)])
        )
    attn_out = heads_to_tokens(all_back[0], head_slots, token_count, head_count, head_dim)
    query_grad = heads_to_tokens(all_back[1], head_slots, token_count, head_count, head_dim)
    key_grad = heads_to_tokens(all_back[2], head_slots, token_count, head_count, head_dim)
    value_grad = heads_to_tokens(all_back[3], head_slots, token_count, head_count, head_dim)
    return (attn_out, query_grad, key_grad, value_grad, weight_grad)


def solution(mesh):
    placed = (
        P("dp", "seq", None),
        P("dp", "seq", None),
        P("dp", "seq", None),
        P("dp", "seq", None),
        P("seq", None, "dp"),
        P(),
        P(),
    )
    return jax.shard_map(
        on_device,
        mesh=mesh,
        in_specs=placed,
        out_specs=(
            P("dp", "seq", None),
            P("dp", "seq", None),
            P("dp", "seq", None),
            P("dp", "seq", None),
            P("seq", None, "dp"),
        ),
        check_vma=False,
    )
```

```python
import jax
import jax.numpy as jnp
from jax import lax
from jax.sharding import PartitionSpec as P
import functools
from jax.experimental import pallas as pl
from jax.experimental.pallas import tpu as pltpu


TILE = 128
NT = (((1,), (1,)), ((), ()))
TN = (((0,), (0,)), ((), ()))


def _probs(q, k, bias, scale):
    sc = lax.dot_general(q, k, NT, preferred_element_type=jnp.float32) * scale + bias
    e = jnp.exp(sc - jnp.max(sc, axis=1, keepdims=True))
    return e / jnp.sum(e, axis=1, keepdims=True)


def _fwd_kernel(q_ref, k_ref, v_ref, b_ref, o_ref, p_ref, *, scale):
    prob = _probs(q_ref[0], k_ref[0], b_ref[0, 0], scale)
    p_ref[0] = prob.T
    out = jnp.dot(prob.astype(jnp.bfloat16), v_ref[0], preferred_element_type=jnp.float32)
    o_ref[0] = out.astype(o_ref.dtype)


def _bwd_kernel(q_ref, k_ref, v_ref, p_ref, o_ref, do_ref, dq_ref, dk_ref, dv_ref,
                dk_scr, dv_scr, *, nb, scale):
    qi = pl.program_id(0)

    @pl.when(qi == 0)
    def _():
        dk_scr[...] = jnp.zeros(dk_scr.shape, jnp.float32)
        dv_scr[...] = jnp.zeros(dv_scr.shape, jnp.float32)

    q = q_ref[0]
    k = k_ref[0]
    v = v_ref[0]
    do = do_ref[0]
    prob_t = p_ref[0]
    low_t = prob_t.astype(jnp.bfloat16)
    product = do.astype(jnp.float32) * o_ref[0].astype(jnp.float32)
    delta_row = jnp.sum(product.T, axis=0, keepdims=True)
    dv_scr[...] += jnp.dot(low_t, do, preferred_element_type=jnp.float32)
    dp_t = lax.dot_general(v, do, NT, preferred_element_type=jnp.float32)
    ds_t = (prob_t * (dp_t - delta_row) * scale).astype(jnp.bfloat16)
    dq_ref[0] = lax.dot_general(ds_t, k, TN, preferred_element_type=jnp.float32).astype(dq_ref.dtype)
    dk_scr[...] += jnp.dot(ds_t, q, preferred_element_type=jnp.float32)

    @pl.when(qi == nb - 1)
    def _():
        dk_ref[0] = dk_scr[...].astype(dk_ref.dtype)
        dv_ref[0] = dv_scr[...].astype(dv_ref.dtype)


def mask_bias(slot_mask, length):
    spread = jnp.repeat(slot_mask, length // slot_mask.shape[2], axis=2)
    return jnp.where(spread > 0, 0.0, -jnp.inf).astype(jnp.float32)[:, :, None, :]


def attn_forward(bias, q, k, v, scale):
    slots, length, hd = q.shape
    nb = length // TILE
    row = pl.BlockSpec((1, TILE, hd), lambda s, i: (s, i, 0))
    full = pl.BlockSpec((1, length, hd), lambda s, i: (s, 0, 0))
    brow = pl.BlockSpec((1, 1, 1, length), lambda s, i: (s, i, 0, 0))
    prow = pl.BlockSpec((1, length, TILE), lambda s, i: (s, 0, i))
    return pl.pallas_call(
        functools.partial(_fwd_kernel, scale=scale),
        grid=(slots, nb),
        in_specs=[row, full, full, brow],
        out_specs=[row, prow],
        out_shape=(
            jax.ShapeDtypeStruct(q.shape, jnp.bfloat16),
            jax.ShapeDtypeStruct((slots, length, length), jnp.float32),
        ),
        compiler_params=pltpu.CompilerParams(dimension_semantics=("arbitrary", "arbitrary")),
    )(q, k, v, bias)


def attn_backward(prob, q, k, v, o, do, scale, slot):
    slots, length, hd = q.shape
    nb = length // TILE
    row = pl.BlockSpec((1, TILE, hd), lambda i: (slot, i, 0))
    full = pl.BlockSpec((1, length, hd), lambda i: (slot, 0, 0))
    prow = pl.BlockSpec((1, length, TILE), lambda i: (slot, 0, i))
    out_row = pl.BlockSpec((1, TILE, hd), lambda i: (0, i, 0))
    out_full = pl.BlockSpec((1, length, hd), lambda i: (0, 0, 0))
    shape = jax.ShapeDtypeStruct((1, length, hd), jnp.bfloat16)
    return pl.pallas_call(
        functools.partial(_bwd_kernel, nb=nb, scale=scale),
        grid=(nb,),
        in_specs=[row, full, full, prow, row, row],
        out_specs=[out_row, out_full, out_full],
        out_shape=(shape, shape, shape),
        scratch_shapes=[pltpu.VMEM((length, hd), jnp.float32), pltpu.VMEM((length, hd), jnp.float32)],
        compiler_params=pltpu.CompilerParams(dimension_semantics=("arbitrary",)),
    )(q, k, v, prob, o, do)


def slot_table(head_owner, most_slots, seq_count):
    head_count = head_owner.shape[0]
    same_owner = head_owner[:, None] == head_owner[None, :]
    earlier = jnp.arange(head_count)[None, :] < jnp.arange(head_count)[:, None]
    owner_rank = jnp.sum(jnp.logical_and(same_owner, earlier), axis=1)
    slot_index = head_owner * most_slots + owner_rank
    return slot_index[:, None] == jnp.arange(seq_count * most_slots, dtype=jnp.int32)[None, :]


def heads_to_tokens(received, head_slots, token_count, head_count, head_dim):
    picked = jnp.take(received[:, 0], head_slots, axis=0)
    return jnp.transpose(picked, (1, 0, 2)).reshape(1, token_count, head_count * head_dim)


def on_device(query_tok, key_tok, value_tok, grad_out, out_weight, block_mask, head_owner):
    seq_count = lax.axis_size("seq")
    most_slots = out_weight.shape[0]
    head_dim = out_weight.shape[1]
    token_count = query_tok.shape[1]
    head_count = block_mask.shape[0]
    length = seq_count * token_count
    score_scale = head_dim ** (-0.5)
    grad_scale = (lax.axis_size("dp") * length) ** (-0.5)
    table = slot_table(head_owner, most_slots, seq_count)
    head_slots = jnp.argmax(table, axis=1).astype(jnp.int32)
    select = table.astype(jnp.bfloat16)
    my_first = lax.axis_index("seq") * most_slots
    local_select = lax.dynamic_slice_in_dim(table.astype(jnp.float32), my_first, most_slots, 1)
    slot_blocks = jnp.einsum("hs,hab->sab", local_select, block_mask.astype(jnp.float32))
    slot_used = jnp.sum(local_select, axis=0)
    diagonal = jnp.eye(block_mask.shape[1], dtype=jnp.float32)
    slot_blocks = slot_blocks + (1.0 - slot_used)[:, None, None] * diagonal[None]
    slot_mask = (slot_blocks > 0.5).astype(jnp.int32)
    bias = mask_bias(slot_mask, length)

    def to_slots(tensor):
        split_heads = tensor[0].reshape(token_count, head_count, head_dim)
        spread = jnp.einsum("thd,hj->jtd", split_heads, select, preferred_element_type=jnp.float32)
        return spread.astype(jnp.bfloat16).reshape(seq_count, most_slots, token_count, head_dim)

    stacked = jnp.stack([to_slots(query_tok), to_slots(key_tok), to_slots(value_tok)], axis=1)
    arrived = lax.all_to_all(stacked, "seq", split_axis=0, concat_axis=3, tiled=True)[0]
    slot_query = arrived[0]
    slot_key = arrived[1]
    slot_value = arrived[2]
    dp_count = lax.axis_size("dp")
    weight_copies = jnp.broadcast_to(out_weight[None], (dp_count,) + out_weight.shape)
    weight_parts = lax.all_to_all(weight_copies, "dp", split_axis=0, concat_axis=0, tiled=True)
    slot_out, slot_prob = attn_forward(bias, slot_query, slot_key, slot_value, score_scale)

    def back_layout(stacked):
        return stacked.reshape(most_slots, seq_count, token_count, head_dim)

    weight_full = jnp.transpose(weight_parts, (1, 2, 0, 3)).reshape(
        most_slots, head_dim, dp_count * out_weight.shape[2]
    )
    dy_rows = lax.all_gather(grad_out, "seq", axis=1, tiled=True)[0]
    part = jnp.einsum(
        "td,shd->sth", dy_rows, weight_full, preferred_element_type=jnp.float32
    ).astype(jnp.bfloat16)
    grad_attn = part
    weight_total = jnp.einsum("sth,td->shd", slot_out, dy_rows, preferred_element_type=jnp.float32)
    grad_attn, weight_total = lax.optimization_barrier((grad_attn, weight_total))
    weight_grad = lax.psum_scatter(
        (weight_total * grad_scale).astype(jnp.bfloat16), "dp", scatter_dimension=2, tiled=True
    ).astype(jnp.float32)
    def to_owners(tensors):
        one_stack = jnp.stack([t.reshape(seq_count, token_count, head_dim) for t in tensors])
        return lax.all_to_all(one_stack, "seq", split_axis=1, concat_axis=1, tiled=True)

    sent = []
    for slot_number in range(most_slots):
        slot_grads = attn_backward(
            slot_prob, slot_query, slot_key, slot_value, slot_out, grad_attn, score_scale, slot_number
        )
        if slot_number == 0:
            sent.append(to_owners(tuple(slot_out) + tuple(slot_grads)))
        else:
            sent.append(to_owners(slot_grads))
    base = most_slots

    def merged(pieces):
        return jnp.stack(pieces, axis=1).reshape(seq_count * most_slots, 1, token_count, head_dim)

    all_back = [merged([sent[0][number] for number in range(most_slots)])]
    for which in range(3):
        all_back.append(
            merged([sent[0][base + which]] + [sent[number][which] for number in range(1, most_slots)])
        )
    attn_out = heads_to_tokens(all_back[0], head_slots, token_count, head_count, head_dim)
    query_grad = heads_to_tokens(all_back[1], head_slots, token_count, head_count, head_dim)
    key_grad = heads_to_tokens(all_back[2], head_slots, token_count, head_count, head_dim)
    value_grad = heads_to_tokens(all_back[3], head_slots, token_count, head_count, head_dim)
    return (attn_out, query_grad, key_grad, value_grad, weight_grad)


def solution(mesh):
    placed = (
        P("dp", "seq", None),
        P("dp", "seq", None),
        P("dp", "seq", None),
        P("dp", "seq", None),
        P("seq", None, "dp"),
        P(),
        P(),
    )
    return jax.shard_map(
        on_device,
        mesh=mesh,
        in_specs=placed,
        out_specs=(
            P("dp", "seq", None),
            P("dp", "seq", None),
            P("dp", "seq", None),
            P("dp", "seq", None),
            P("seq", None, "dp"),
        ),
        check_vma=False,
    )
```

```python
import jax
import jax.numpy as jnp
from jax import lax
from jax.sharding import PartitionSpec as P
import functools
from jax.experimental import pallas as pl
from jax.experimental.pallas import tpu as pltpu


TILE = 128
NT = (((1,), (1,)), ((), ()))
TN = (((0,), (0,)), ((), ()))


def _probs(q, k, bias, scale):
    sc = lax.dot_general(q, k, NT, preferred_element_type=jnp.float32) * scale + bias
    e = jnp.exp(sc - jnp.max(sc, axis=1, keepdims=True))
    return e / jnp.sum(e, axis=1, keepdims=True)


def _fwd_kernel(q_ref, k_ref, v_ref, b_ref, o_ref, p_ref, *, scale):
    prob = _probs(q_ref[0], k_ref[0], b_ref[0, 0], scale)
    p_ref[0] = prob.T
    out = jnp.dot(prob.astype(jnp.bfloat16), v_ref[0], preferred_element_type=jnp.float32)
    o_ref[0] = out.astype(o_ref.dtype)


def _bwd_kernel(q_ref, k_ref, v_ref, p_ref, o_ref, do_ref, dq_ref, dk_ref, dv_ref,
                dk_scr, dv_scr, *, nb, scale):
    qi = pl.program_id(0)

    @pl.when(qi == 0)
    def _():
        dk_scr[...] = jnp.zeros(dk_scr.shape, jnp.float32)
        dv_scr[...] = jnp.zeros(dv_scr.shape, jnp.float32)

    q = q_ref[0]
    k = k_ref[0]
    v = v_ref[0]
    do = do_ref[0]
    prob_t = p_ref[0]
    low_t = prob_t.astype(jnp.bfloat16)
    product = do.astype(jnp.float32) * o_ref[0].astype(jnp.float32)
    delta_row = jnp.sum(product.T, axis=0, keepdims=True)
    dv_scr[...] += jnp.dot(low_t, do, preferred_element_type=jnp.float32)
    dp_t = lax.dot_general(v, do, NT, preferred_element_type=jnp.float32)
    ds_t = (prob_t * (dp_t - delta_row) * scale).astype(jnp.bfloat16)
    dq_ref[0] = lax.dot_general(ds_t, k, TN, preferred_element_type=jnp.float32).astype(dq_ref.dtype)
    dk_scr[...] += jnp.dot(ds_t, q, preferred_element_type=jnp.float32)

    @pl.when(qi == nb - 1)
    def _():
        dk_ref[0] = dk_scr[...].astype(dk_ref.dtype)
        dv_ref[0] = dv_scr[...].astype(dv_ref.dtype)


def mask_bias(slot_mask, length):
    spread = jnp.repeat(slot_mask, length // slot_mask.shape[2], axis=2)
    return jnp.where(spread > 0, 0.0, -jnp.inf).astype(jnp.float32)[:, :, None, :]


def attn_forward(bias, q, k, v, scale):
    slots, length, hd = q.shape
    nb = length // TILE
    row = pl.BlockSpec((1, TILE, hd), lambda s, i: (s, i, 0))
    full = pl.BlockSpec((1, length, hd), lambda s, i: (s, 0, 0))
    brow = pl.BlockSpec((1, 1, 1, length), lambda s, i: (s, i, 0, 0))
    prow = pl.BlockSpec((1, length, TILE), lambda s, i: (s, 0, i))
    return pl.pallas_call(
        functools.partial(_fwd_kernel, scale=scale),
        grid=(slots, nb),
        in_specs=[row, full, full, brow],
        out_specs=[row, prow],
        out_shape=(
            jax.ShapeDtypeStruct(q.shape, jnp.bfloat16),
            jax.ShapeDtypeStruct((slots, length, length), jnp.float32),
        ),
        compiler_params=pltpu.CompilerParams(dimension_semantics=("arbitrary", "arbitrary")),
    )(q, k, v, bias)


def attn_backward(prob, q, k, v, o, do, scale, slot):
    slots, length, hd = q.shape
    nb = length // TILE
    row = pl.BlockSpec((1, TILE, hd), lambda i: (slot, i, 0))
    full = pl.BlockSpec((1, length, hd), lambda i: (slot, 0, 0))
    prow = pl.BlockSpec((1, length, TILE), lambda i: (slot, 0, i))
    out_row = pl.BlockSpec((1, TILE, hd), lambda i: (0, i, 0))
    out_full = pl.BlockSpec((1, length, hd), lambda i: (0, 0, 0))
    shape = jax.ShapeDtypeStruct((1, length, hd), jnp.bfloat16)
    return pl.pallas_call(
        functools.partial(_bwd_kernel, nb=nb, scale=scale),
        grid=(nb,),
        in_specs=[row, full, full, prow, row, row],
        out_specs=[out_row, out_full, out_full],
        out_shape=(shape, shape, shape),
        scratch_shapes=[pltpu.VMEM((length, hd), jnp.float32), pltpu.VMEM((length, hd), jnp.float32)],
        compiler_params=pltpu.CompilerParams(dimension_semantics=("arbitrary",)),
    )(q, k, v, prob, o, do)


def slot_table(head_owner, most_slots, seq_count):
    head_count = head_owner.shape[0]
    same_owner = head_owner[:, None] == head_owner[None, :]
    earlier = jnp.arange(head_count)[None, :] < jnp.arange(head_count)[:, None]
    owner_rank = jnp.sum(jnp.logical_and(same_owner, earlier), axis=1)
    slot_index = head_owner * most_slots + owner_rank
    return slot_index[:, None] == jnp.arange(seq_count * most_slots, dtype=jnp.int32)[None, :]


def heads_to_tokens(received, head_slots, token_count, head_count, head_dim):
    picked = jnp.take(received[:, 0], head_slots, axis=0)
    return jnp.transpose(picked, (1, 0, 2)).reshape(1, token_count, head_count * head_dim)


def on_device(query_tok, key_tok, value_tok, grad_out, out_weight, block_mask, head_owner):
    seq_count = lax.axis_size("seq")
    most_slots = out_weight.shape[0]
    head_dim = out_weight.shape[1]
    token_count = query_tok.shape[1]
    head_count = block_mask.shape[0]
    length = seq_count * token_count
    score_scale = head_dim ** (-0.5)
    grad_scale = (lax.axis_size("dp") * length) ** (-0.5)
    table = slot_table(head_owner, most_slots, seq_count)
    head_slots = jnp.argmax(table, axis=1).astype(jnp.int32)
    select = table.astype(jnp.bfloat16)
    my_first = lax.axis_index("seq") * most_slots
    local_select = lax.dynamic_slice_in_dim(table.astype(jnp.float32), my_first, most_slots, 1)
    slot_blocks = jnp.einsum("hs,hab->sab", local_select, block_mask.astype(jnp.float32))
    slot_used = jnp.sum(local_select, axis=0)
    diagonal = jnp.eye(block_mask.shape[1], dtype=jnp.float32)
    slot_blocks = slot_blocks + (1.0 - slot_used)[:, None, None] * diagonal[None]
    slot_mask = (slot_blocks > 0.5).astype(jnp.int32)
    bias = mask_bias(slot_mask, length)

    def to_slots(tensor):
        split_heads = tensor[0].reshape(token_count, head_count, head_dim)
        spread = jnp.einsum("thd,hj->jtd", split_heads, select, preferred_element_type=jnp.float32)
        return spread.astype(jnp.bfloat16).reshape(seq_count, most_slots, token_count, head_dim)

    stacked = jnp.stack([to_slots(query_tok), to_slots(key_tok), to_slots(value_tok)], axis=1)
    arrived = lax.all_to_all(stacked, "seq", split_axis=0, concat_axis=3, tiled=True)[0]
    slot_query = arrived[0]
    slot_key = arrived[1]
    slot_value = arrived[2]
    dp_count = lax.axis_size("dp")
    weight_copies = jnp.broadcast_to(out_weight[None], (dp_count,) + out_weight.shape)
    weight_parts = lax.all_to_all(weight_copies, "dp", split_axis=0, concat_axis=0, tiled=True)
    slot_out, slot_prob = attn_forward(bias, slot_query, slot_key, slot_value, score_scale)

    def back_layout(stacked):
        return stacked.reshape(most_slots, seq_count, token_count, head_dim)

    weight_full = jnp.transpose(weight_parts, (1, 2, 0, 3)).reshape(
        most_slots, head_dim, dp_count * out_weight.shape[2]
    )
    dy_rows = lax.all_gather(grad_out, "seq", axis=1, tiled=True)[0]
    part = jnp.einsum(
        "td,shd->sth", dy_rows, weight_full, preferred_element_type=jnp.float32
    ).astype(jnp.bfloat16)
    grad_attn = part
    weight_total = jnp.einsum("td,sth->dsh", dy_rows, slot_out, preferred_element_type=jnp.float32)
    grad_attn, weight_total = lax.optimization_barrier((grad_attn, weight_total))
    weight_rows = lax.psum_scatter(
        (weight_total * grad_scale).astype(jnp.bfloat16), "dp", scatter_dimension=0, tiled=True
    )
    weight_grad = jnp.transpose(weight_rows, (1, 2, 0)).astype(jnp.float32)
    def to_owners(tensors):
        one_stack = jnp.stack([t.reshape(seq_count, token_count, head_dim) for t in tensors])
        return lax.all_to_all(one_stack, "seq", split_axis=1, concat_axis=1, tiled=True)

    sent = []
    for slot_number in range(most_slots):
        slot_grads = attn_backward(
            slot_prob, slot_query, slot_key, slot_value, slot_out, grad_attn, score_scale, slot_number
        )
        if slot_number == 0:
            sent.append(to_owners(tuple(slot_out) + tuple(slot_grads)))
        else:
            sent.append(to_owners(slot_grads))
    base = most_slots

    def merged(pieces):
        return jnp.stack(pieces, axis=1).reshape(seq_count * most_slots, 1, token_count, head_dim)

    all_back = [merged([sent[0][number] for number in range(most_slots)])]
    for which in range(3):
        all_back.append(
            merged([sent[0][base + which]] + [sent[number][which] for number in range(1, most_slots)])
        )
    attn_out = heads_to_tokens(all_back[0], head_slots, token_count, head_count, head_dim)
    query_grad = heads_to_tokens(all_back[1], head_slots, token_count, head_count, head_dim)
    key_grad = heads_to_tokens(all_back[2], head_slots, token_count, head_count, head_dim)
    value_grad = heads_to_tokens(all_back[3], head_slots, token_count, head_count, head_dim)
    return (attn_out, query_grad, key_grad, value_grad, weight_grad)


def solution(mesh):
    placed = (
        P("dp", "seq", None),
        P("dp", "seq", None),
        P("dp", "seq", None),
        P("dp", "seq", None),
        P("seq", None, "dp"),
        P(),
        P(),
    )
    return jax.shard_map(
        on_device,
        mesh=mesh,
        in_specs=placed,
        out_specs=(
            P("dp", "seq", None),
            P("dp", "seq", None),
            P("dp", "seq", None),
            P("dp", "seq", None),
            P("seq", None, "dp"),
        ),
        check_vma=False,
    )
```

```python
import jax
import jax.numpy as jnp
from jax import lax
from jax.sharding import PartitionSpec as P
import functools
from jax.experimental import pallas as pl
from jax.experimental.pallas import tpu as pltpu


TILE = 128
NT = (((1,), (1,)), ((), ()))
TN = (((0,), (0,)), ((), ()))


def _probs(q, k, bias, scale):
    sc = lax.dot_general(q, k, NT, preferred_element_type=jnp.float32) * scale + bias
    e = jnp.exp(sc - jnp.max(sc, axis=1, keepdims=True))
    return e / jnp.sum(e, axis=1, keepdims=True)


def _fwd_kernel(q_ref, k_ref, v_ref, b_ref, o_ref, p_ref, *, scale):
    prob = _probs(q_ref[0], k_ref[0], b_ref[0, 0], scale)
    p_ref[0] = prob.T
    out = jnp.dot(prob.astype(jnp.bfloat16), v_ref[0], preferred_element_type=jnp.float32)
    o_ref[0] = out.astype(o_ref.dtype)


def _bwd_kernel(q_ref, k_ref, v_ref, p_ref, o_ref, do_ref, g_ref, dk_scr, dv_scr, *, nb, scale):
    qi = pl.program_id(0)

    @pl.when(qi == 0)
    def _():
        dk_scr[...] = jnp.zeros(dk_scr.shape, jnp.float32)
        dv_scr[...] = jnp.zeros(dv_scr.shape, jnp.float32)

    q = q_ref[0]
    k = k_ref[0]
    v = v_ref[0]
    do = do_ref[0]
    prob_t = p_ref[0]
    low_t = prob_t.astype(jnp.bfloat16)
    product = do.astype(jnp.float32) * o_ref[0].astype(jnp.float32)
    delta_row = jnp.sum(product.T, axis=0, keepdims=True)
    dv_scr[...] += jnp.dot(low_t, do, preferred_element_type=jnp.float32)
    dp_t = lax.dot_general(v, do, NT, preferred_element_type=jnp.float32)
    ds_t = (prob_t * (dp_t - delta_row) * scale).astype(jnp.bfloat16)
    row_first = pl.multiple_of(qi * TILE, TILE)
    dq = lax.dot_general(ds_t, k, TN, preferred_element_type=jnp.float32)
    g_ref[0, pl.ds(row_first, TILE), :] = dq.astype(g_ref.dtype)
    dk_scr[...] += jnp.dot(ds_t, q, preferred_element_type=jnp.float32)

    @pl.when(qi == nb - 1)
    def _():
        g_ref[1] = dk_scr[...].astype(g_ref.dtype)
        g_ref[2] = dv_scr[...].astype(g_ref.dtype)


def mask_bias(slot_mask, length):
    spread = jnp.repeat(slot_mask, length // slot_mask.shape[2], axis=2)
    return jnp.where(spread > 0, 0.0, -jnp.inf).astype(jnp.float32)[:, :, None, :]


def attn_forward(bias, q, k, v, scale):
    slots, length, hd = q.shape
    nb = length // TILE
    row = pl.BlockSpec((1, TILE, hd), lambda s, i: (s, i, 0))
    full = pl.BlockSpec((1, length, hd), lambda s, i: (s, 0, 0))
    brow = pl.BlockSpec((1, 1, 1, length), lambda s, i: (s, i, 0, 0))
    prow = pl.BlockSpec((1, length, TILE), lambda s, i: (s, 0, i))
    return pl.pallas_call(
        functools.partial(_fwd_kernel, scale=scale),
        grid=(slots, nb),
        in_specs=[row, full, full, brow],
        out_specs=[row, prow],
        out_shape=(
            jax.ShapeDtypeStruct(q.shape, jnp.bfloat16),
            jax.ShapeDtypeStruct((slots, length, length), jnp.float32),
        ),
        compiler_params=pltpu.CompilerParams(dimension_semantics=("arbitrary", "arbitrary")),
    )(q, k, v, bias)


def attn_backward(prob, q, k, v, o, do, scale, slot):
    slots, length, hd = q.shape
    nb = length // TILE
    row = pl.BlockSpec((1, TILE, hd), lambda i: (slot, i, 0))
    full = pl.BlockSpec((1, length, hd), lambda i: (slot, 0, 0))
    prow = pl.BlockSpec((1, length, TILE), lambda i: (slot, 0, i))
    stacked = pl.BlockSpec((3, length, hd), lambda i: (0, 0, 0))
    return pl.pallas_call(
        functools.partial(_bwd_kernel, nb=nb, scale=scale),
        grid=(nb,),
        in_specs=[row, full, full, prow, row, row],
        out_specs=stacked,
        out_shape=jax.ShapeDtypeStruct((3, length, hd), jnp.bfloat16),
        scratch_shapes=[pltpu.VMEM((length, hd), jnp.float32), pltpu.VMEM((length, hd), jnp.float32)],
        compiler_params=pltpu.CompilerParams(dimension_semantics=("arbitrary",)),
    )(q, k, v, prob, o, do)


def slot_table(head_owner, most_slots, seq_count):
    head_count = head_owner.shape[0]
    same_owner = head_owner[:, None] == head_owner[None, :]
    earlier = jnp.arange(head_count)[None, :] < jnp.arange(head_count)[:, None]
    owner_rank = jnp.sum(jnp.logical_and(same_owner, earlier), axis=1)
    slot_index = head_owner * most_slots + owner_rank
    return slot_index[:, None] == jnp.arange(seq_count * most_slots, dtype=jnp.int32)[None, :]


def heads_to_tokens(received, head_slots, token_count, head_count, head_dim):
    picked = jnp.take(received[:, 0], head_slots, axis=0)
    return jnp.transpose(picked, (1, 0, 2)).reshape(1, token_count, head_count * head_dim)


def on_device(query_tok, key_tok, value_tok, grad_out, out_weight, block_mask, head_owner):
    seq_count = lax.axis_size("seq")
    most_slots = out_weight.shape[0]
    head_dim = out_weight.shape[1]
    token_count = query_tok.shape[1]
    head_count = block_mask.shape[0]
    length = seq_count * token_count
    score_scale = head_dim ** (-0.5)
    grad_scale = (lax.axis_size("dp") * length) ** (-0.5)
    table = slot_table(head_owner, most_slots, seq_count)
    head_slots = jnp.argmax(table, axis=1).astype(jnp.int32)
    select = table.astype(jnp.bfloat16)
    my_first = lax.axis_index("seq") * most_slots
    local_select = lax.dynamic_slice_in_dim(table.astype(jnp.float32), my_first, most_slots, 1)
    slot_blocks = jnp.einsum("hs,hab->sab", local_select, block_mask.astype(jnp.float32))
    slot_used = jnp.sum(local_select, axis=0)
    diagonal = jnp.eye(block_mask.shape[1], dtype=jnp.float32)
    slot_blocks = slot_blocks + (1.0 - slot_used)[:, None, None] * diagonal[None]
    slot_mask = (slot_blocks > 0.5).astype(jnp.int32)
    bias = mask_bias(slot_mask, length)

    def to_slots(tensor):
        split_heads = tensor[0].reshape(token_count, head_count, head_dim)
        spread = jnp.einsum("thd,hj->jtd", split_heads, select, preferred_element_type=jnp.float32)
        return spread.astype(jnp.bfloat16).reshape(seq_count, most_slots, token_count, head_dim)

    stacked = jnp.stack([to_slots(query_tok), to_slots(key_tok), to_slots(value_tok)], axis=1)
    arrived = lax.all_to_all(stacked, "seq", split_axis=0, concat_axis=3, tiled=True)[0]
    slot_query = arrived[0]
    slot_key = arrived[1]
    slot_value = arrived[2]
    dp_count = lax.axis_size("dp")
    weight_copies = jnp.broadcast_to(out_weight[None], (dp_count,) + out_weight.shape)
    weight_parts = lax.all_to_all(weight_copies, "dp", split_axis=0, concat_axis=0, tiled=True)
    slot_out, slot_prob = attn_forward(bias, slot_query, slot_key, slot_value, score_scale)

    def back_layout(stacked):
        return stacked.reshape(most_slots, seq_count, token_count, head_dim)

    out_back = lax.all_to_all(back_layout(slot_out), "seq", split_axis=1, concat_axis=0, tiled=True)

    weight_full = jnp.transpose(weight_parts, (1, 2, 0, 3)).reshape(
        most_slots, head_dim, dp_count * out_weight.shape[2]
    )
    dy_rows = lax.all_gather(grad_out, "seq", axis=1, tiled=True)[0]
    part = jnp.einsum(
        "td,shd->sth", dy_rows, weight_full, preferred_element_type=jnp.float32
    ).astype(jnp.bfloat16)
    grad_attn = part
    weight_total = jnp.einsum("td,sth->dsh", dy_rows, slot_out, preferred_element_type=jnp.float32)
    grad_attn, weight_total = lax.optimization_barrier((grad_attn, weight_total))
    weight_rows = lax.psum_scatter(
        (weight_total * grad_scale).astype(jnp.bfloat16), "dp", scatter_dimension=0, tiled=True
    )
    weight_grad = jnp.transpose(weight_rows, (1, 2, 0)).astype(jnp.float32)
    def to_owners(one_stack):
        return lax.all_to_all(one_stack, "seq", split_axis=1, concat_axis=1, tiled=True)

    sent = []
    for slot_number in range(most_slots):
        slot_grads = attn_backward(
            slot_prob, slot_query, slot_key, slot_value, slot_out, grad_attn, score_scale, slot_number
        ).reshape(3, seq_count, token_count, head_dim)
        sent.append(to_owners(slot_grads))
    def merged(pieces):
        return jnp.stack(pieces, axis=1).reshape(seq_count * most_slots, 1, token_count, head_dim)

    all_back = [out_back]
    for which in range(3):
        all_back.append(merged([sent[number][which] for number in range(most_slots)]))
    attn_out = heads_to_tokens(all_back[0], head_slots, token_count, head_count, head_dim)
    query_grad = heads_to_tokens(all_back[1], head_slots, token_count, head_count, head_dim)
    key_grad = heads_to_tokens(all_back[2], head_slots, token_count, head_count, head_dim)
    value_grad = heads_to_tokens(all_back[3], head_slots, token_count, head_count, head_dim)
    return (attn_out, query_grad, key_grad, value_grad, weight_grad)


def solution(mesh):
    placed = (
        P("dp", "seq", None),
        P("dp", "seq", None),
        P("dp", "seq", None),
        P("dp", "seq", None),
        P("seq", None, "dp"),
        P(),
        P(),
    )
    return jax.shard_map(
        on_device,
        mesh=mesh,
        in_specs=placed,
        out_specs=(
            P("dp", "seq", None),
            P("dp", "seq", None),
            P("dp", "seq", None),
            P("dp", "seq", None),
            P("seq", None, "dp"),
        ),
        check_vma=False,
    )
```

```python
import jax
import jax.numpy as jnp
from jax import lax
from jax.sharding import PartitionSpec as P
import functools
from jax.experimental import pallas as pl
from jax.experimental.pallas import tpu as pltpu


TILE = 128
NT = (((1,), (1,)), ((), ()))
TN = (((0,), (0,)), ((), ()))


def _probs(q, k, bias, scale):
    sc = lax.dot_general(q, k, NT, preferred_element_type=jnp.float32) * scale + bias
    e = jnp.exp(sc - jnp.max(sc, axis=1, keepdims=True))
    return e / jnp.sum(e, axis=1, keepdims=True)


def _fwd_kernel(q_ref, k_ref, v_ref, b_ref, o_ref, p_ref, *, scale):
    prob = _probs(q_ref[0], k_ref[0], b_ref[0, 0], scale)
    p_ref[0] = prob.T
    out = jnp.dot(prob.astype(jnp.bfloat16), v_ref[0], preferred_element_type=jnp.float32)
    o_ref[0] = out.astype(o_ref.dtype)


def _bwd_kernel(q_ref, k_ref, v_ref, p_ref, o_ref, do_ref, g_ref, dk_scr, dv_scr, *, nb, scale):
    qi = pl.program_id(0)

    @pl.when(qi == 0)
    def _():
        dk_scr[...] = jnp.zeros(dk_scr.shape, jnp.float32)
        dv_scr[...] = jnp.zeros(dv_scr.shape, jnp.float32)

    q = q_ref[0]
    k = k_ref[0]
    v = v_ref[0]
    do = do_ref[0]
    prob_t = p_ref[0]
    low_t = prob_t.astype(jnp.bfloat16)
    product = do.astype(jnp.float32) * o_ref[0].astype(jnp.float32)
    delta_row = jnp.sum(product.T, axis=0, keepdims=True)
    dv_scr[...] += jnp.dot(low_t, do, preferred_element_type=jnp.float32)
    dp_t = lax.dot_general(v, do, NT, preferred_element_type=jnp.float32)
    ds_t = (prob_t * (dp_t - delta_row) * scale).astype(jnp.bfloat16)
    dq = lax.dot_general(ds_t, k, TN, preferred_element_type=jnp.float32)
    g_ref[qi, 0] = dq.astype(g_ref.dtype)
    dk_scr[...] += jnp.dot(ds_t, q, preferred_element_type=jnp.float32)

    @pl.when(qi == nb - 1)
    def _():
        g_ref[:, 1] = dk_scr[...].reshape(nb, TILE, dk_scr.shape[1]).astype(g_ref.dtype)
        g_ref[:, 2] = dv_scr[...].reshape(nb, TILE, dv_scr.shape[1]).astype(g_ref.dtype)


def mask_bias(slot_mask, length):
    spread = jnp.repeat(slot_mask, length // slot_mask.shape[2], axis=2)
    return jnp.where(spread > 0, 0.0, -jnp.inf).astype(jnp.float32)[:, :, None, :]


def attn_forward(bias, q, k, v, scale):
    slots, length, hd = q.shape
    nb = length // TILE
    row = pl.BlockSpec((1, TILE, hd), lambda s, i: (s, i, 0))
    full = pl.BlockSpec((1, length, hd), lambda s, i: (s, 0, 0))
    brow = pl.BlockSpec((1, 1, 1, length), lambda s, i: (s, i, 0, 0))
    prow = pl.BlockSpec((1, length, TILE), lambda s, i: (s, 0, i))
    return pl.pallas_call(
        functools.partial(_fwd_kernel, scale=scale),
        grid=(slots, nb),
        in_specs=[row, full, full, brow],
        out_specs=[row, prow],
        out_shape=(
            jax.ShapeDtypeStruct(q.shape, jnp.bfloat16),
            jax.ShapeDtypeStruct((slots, length, length), jnp.float32),
        ),
        compiler_params=pltpu.CompilerParams(dimension_semantics=("arbitrary", "arbitrary")),
    )(q, k, v, bias)


def attn_backward(prob, q, k, v, o, do, scale, slot):
    slots, length, hd = q.shape
    nb = length // TILE
    row = pl.BlockSpec((1, TILE, hd), lambda i: (slot, i, 0))
    full = pl.BlockSpec((1, length, hd), lambda i: (slot, 0, 0))
    prow = pl.BlockSpec((1, length, TILE), lambda i: (slot, 0, i))
    stacked = pl.BlockSpec((nb, 3, TILE, hd), lambda i: (0, 0, 0, 0))
    return pl.pallas_call(
        functools.partial(_bwd_kernel, nb=nb, scale=scale),
        grid=(nb,),
        in_specs=[row, full, full, prow, row, row],
        out_specs=stacked,
        out_shape=jax.ShapeDtypeStruct((nb, 3, TILE, hd), jnp.bfloat16),
        scratch_shapes=[pltpu.VMEM((length, hd), jnp.float32), pltpu.VMEM((length, hd), jnp.float32)],
        compiler_params=pltpu.CompilerParams(dimension_semantics=("arbitrary",)),
    )(q, k, v, prob, o, do)


def slot_table(head_owner, most_slots, seq_count):
    head_count = head_owner.shape[0]
    same_owner = head_owner[:, None] == head_owner[None, :]
    earlier = jnp.arange(head_count)[None, :] < jnp.arange(head_count)[:, None]
    owner_rank = jnp.sum(jnp.logical_and(same_owner, earlier), axis=1)
    slot_index = head_owner * most_slots + owner_rank
    return slot_index[:, None] == jnp.arange(seq_count * most_slots, dtype=jnp.int32)[None, :]


def heads_to_tokens(received, head_slots, token_count, head_count, head_dim):
    picked = jnp.take(received[:, 0], head_slots, axis=0)
    return jnp.transpose(picked, (1, 0, 2)).reshape(1, token_count, head_count * head_dim)


def on_device(query_tok, key_tok, value_tok, grad_out, out_weight, block_mask, head_owner):
    seq_count = lax.axis_size("seq")
    most_slots = out_weight.shape[0]
    head_dim = out_weight.shape[1]
    token_count = query_tok.shape[1]
    head_count = block_mask.shape[0]
    length = seq_count * token_count
    score_scale = head_dim ** (-0.5)
    grad_scale = (lax.axis_size("dp") * length) ** (-0.5)
    table = slot_table(head_owner, most_slots, seq_count)
    head_slots = jnp.argmax(table, axis=1).astype(jnp.int32)
    select = table.astype(jnp.bfloat16)
    my_first = lax.axis_index("seq") * most_slots
    local_select = lax.dynamic_slice_in_dim(table.astype(jnp.float32), my_first, most_slots, 1)
    slot_blocks = jnp.einsum("hs,hab->sab", local_select, block_mask.astype(jnp.float32))
    slot_used = jnp.sum(local_select, axis=0)
    diagonal = jnp.eye(block_mask.shape[1], dtype=jnp.float32)
    slot_blocks = slot_blocks + (1.0 - slot_used)[:, None, None] * diagonal[None]
    slot_mask = (slot_blocks > 0.5).astype(jnp.int32)
    bias = mask_bias(slot_mask, length)

    def to_slots(tensor):
        split_heads = tensor[0].reshape(token_count, head_count, head_dim)
        spread = jnp.einsum("thd,hj->jtd", split_heads, select, preferred_element_type=jnp.float32)
        return spread.astype(jnp.bfloat16).reshape(seq_count, most_slots, token_count, head_dim)

    stacked = jnp.stack([to_slots(query_tok), to_slots(key_tok), to_slots(value_tok)], axis=1)
    arrived = lax.all_to_all(stacked, "seq", split_axis=0, concat_axis=3, tiled=True)[0]
    slot_query = arrived[0]
    slot_key = arrived[1]
    slot_value = arrived[2]
    dp_count = lax.axis_size("dp")
    weight_copies = jnp.broadcast_to(out_weight[None], (dp_count,) + out_weight.shape)
    weight_parts = lax.all_to_all(weight_copies, "dp", split_axis=0, concat_axis=0, tiled=True)
    slot_out, slot_prob = attn_forward(bias, slot_query, slot_key, slot_value, score_scale)

    def back_layout(stacked):
        return stacked.reshape(most_slots, seq_count, token_count, head_dim)

    out_back = lax.all_to_all(back_layout(slot_out), "seq", split_axis=1, concat_axis=0, tiled=True)

    weight_full = jnp.transpose(weight_parts, (1, 2, 0, 3)).reshape(
        most_slots, head_dim, dp_count * out_weight.shape[2]
    )
    dy_rows = lax.all_gather(grad_out, "seq", axis=1, tiled=True)[0]
    part = jnp.einsum(
        "td,shd->sth", dy_rows, weight_full, preferred_element_type=jnp.float32
    ).astype(jnp.bfloat16)
    grad_attn = part
    weight_total = jnp.einsum("td,sth->dsh", dy_rows, slot_out, preferred_element_type=jnp.float32)
    grad_attn, weight_total = lax.optimization_barrier((grad_attn, weight_total))
    weight_rows = lax.psum_scatter(
        (weight_total * grad_scale).astype(jnp.bfloat16), "dp", scatter_dimension=0, tiled=True
    )
    weight_grad = jnp.transpose(weight_rows, (1, 2, 0)).astype(jnp.float32)
    def to_owners(one_stack):
        return lax.all_to_all(one_stack, "seq", split_axis=1, concat_axis=1, tiled=True)

    sent = []
    for slot_number in range(most_slots):
        slot_grads = attn_backward(
            slot_prob, slot_query, slot_key, slot_value, slot_out, grad_attn, score_scale, slot_number
        ).transpose(1, 0, 2, 3)
        sent.append(to_owners(slot_grads))
    def merged(pieces):
        return jnp.stack(pieces, axis=1).reshape(seq_count * most_slots, 1, token_count, head_dim)

    all_back = [out_back]
    for which in range(3):
        all_back.append(merged([sent[number][which] for number in range(most_slots)]))
    attn_out = heads_to_tokens(all_back[0], head_slots, token_count, head_count, head_dim)
    query_grad = heads_to_tokens(all_back[1], head_slots, token_count, head_count, head_dim)
    key_grad = heads_to_tokens(all_back[2], head_slots, token_count, head_count, head_dim)
    value_grad = heads_to_tokens(all_back[3], head_slots, token_count, head_count, head_dim)
    return (attn_out, query_grad, key_grad, value_grad, weight_grad)


def solution(mesh):
    placed = (
        P("dp", "seq", None),
        P("dp", "seq", None),
        P("dp", "seq", None),
        P("dp", "seq", None),
        P("seq", None, "dp"),
        P(),
        P(),
    )
    return jax.shard_map(
        on_device,
        mesh=mesh,
        in_specs=placed,
        out_specs=(
            P("dp", "seq", None),
            P("dp", "seq", None),
            P("dp", "seq", None),
            P("dp", "seq", None),
            P("seq", None, "dp"),
        ),
        check_vma=False,
    )
```
